32 devices in a mesh: gx: 4 (over x, core), gy: 8 (over z, y).
Axes of the slice: x: 2, y: 2, z: 4, core: 2. Of those that a mesh axis runs over, the one named last changes fastest.
Arguments:
- eta: float32 [16, 262144], P(None, ('gx', 'gy')), may hold values from -6 to 6
- forcing: float32 [16, 262144], P(None, ('gx', 'gy')), may hold values from -3 to 3
- couplings: float32 [3, 262144], P(None, ('gx', 'gy')), may hold values from 0.02 to 0.3
- neighbors: int32 [3, 262144], P(None, ('gx', 'gy')), may hold values from 0 to 8703, as said below
- halo_send: int32 [32, 512], P(('gx', 'gy')), may hold values from 0 to 8191
- cycle_send: int32 [32, 32, 512], P(('gx', 'gy')), may hold values from 0 to 8191
- stencil: int32 [3, 2097152], P(None, ('gx', 'gy')), may hold values from 0 to 16383
- stencil_weights: float32 [3, 2097152], P(None, ('gx', 'gy')), as said below
- m_order: int32 [1024], replicated, may hold values from 0 to 1023, as said below
- lat_weights: float32 [1024], replicated, may hold values from 0.5 to 1.5
- love: float32 [1024], replicated, may hold values from 0.1 to 2
- legendre: bfloat16 [1024, 1024, 1024], P(('gx', 'gy')), as said below
Outputs:
- stepped: float32 [16, 262144], P(None, ('gx', 'gy'))
- loading: float32 [16, 262144], P(None, ('gx', 'gy'))
The draws below stay inside these ranges and needn't reach their ends.
Inputs may be any that keep to these rules, and one draw needn't show every extreme that they name: `neighbors`: positions below 8192 are the partition's own cells, the rest its halo cells. `m_order`: each order appears once. legendre[j, l, :] is zero for l < m_order[j]. `stencil_weights`: the 3 weights of a grid point are positive and sum to one.
All inputs are finite; a program needn't handle non-finite values.
Results may differ from the reference program's by a relative error of at most 0.0044.
Values may be sent and summed in bfloat16 or wider, within the bound.
No kernel may reach another device: no remote copies, remote signals or barrier semaphores. Data moves between devices by JAX's collectives and lax.ppermute only.
A program may use at most 320 MiB of HBM per device.

```python
import math
import jax
import jax.numpy as jnp
from jax import lax

NF = 16
CELLS_DEV = 8192
NB = 3
NLAT = 1024
NLON = 2048
DEG = 1024
BAND = 32
HALO = 256
CAP = 512
CELLS = 262144
SLOTS = 16384
CYCLES_DEV = 32
N_GX = 4
N_GY = 8


def order_of(key):
    return jax.random.permutation(jax.random.fold_in(key, 11), DEG).astype(jnp.int32)


def draw_m_order(key, part):
    return order_of(key)


def draw_legendre(key, part):
    order = order_of(key)
    degrees = jnp.arange(DEG, dtype=jnp.int32)
    table_key = jax.random.fold_in(key, 12)

    def one_slot(slot):
        slot_key = jax.random.fold_in(table_key, slot)
        values = jax.random.normal(slot_key, (DEG, NLAT), jnp.float32) / math.sqrt(NLAT)
        live = (degrees >= order[slot]).astype(jnp.float32)
        return (values * live[:, None]).astype(jnp.bfloat16)
    return lax.map(one_slot, jnp.arange(DEG, dtype=jnp.int32))


def draw_neighbors(key, part):
    first, second, third = jax.random.split(key, 3)
    inner = jax.random.randint(first, (NB, CELLS), 0, CELLS_DEV, dtype=jnp.int32)
    outer = jax.random.randint(second, (NB, CELLS), CELLS_DEV, CELLS_DEV + 2 * HALO, dtype=jnp.int32)
    picks = jax.random.randint(third, (NB, CELLS), 0, 8, dtype=jnp.int32)
    chosen = jnp.where(picks == 0, outer, inner)
    return chosen.at[0, 0].set(CELLS_DEV + 2 * HALO - 1)


def draw_stencil_weights(key, part):
    raw = jax.random.uniform(key, (NB, NLAT * NLON), jnp.float32, 0.1, 1.0)
    return raw / jnp.sum(raw, axis=0, keepdims=True)


def touch_ends(entries, stream_key, smallest, high):
    shape = entries.shape
    index_at = [jax.random.randint(jax.random.fold_in(stream_key, axis), (), 0, shape[axis]) for axis in range(len(shape))]
    entries = entries.at[tuple(index_at)].set(smallest)
    longest = shape.index(max(shape))
    index_at[longest] = (index_at[longest] + 1) % shape[longest]
    return entries.at[tuple(index_at)].set(high)


def levels(own_key, extent, cuts, smallest, largest):
    loudness = 1.0
    for dim, parts in cuts:
        draws = jax.random.uniform(jax.random.fold_in(jax.random.fold_in(own_key, 6), dim), (parts,), jnp.float32, smallest / len(cuts), largest / len(cuts))
        loudness = loudness * jnp.repeat(jnp.exp(draws), extent[dim] // parts).reshape((-1,) + (1,) * (len(extent) - 1 - dim))
    return loudness


def normal_values(key, dims, scale, limit, cuts=(), kind=jnp.bfloat16):
    drawn = scale * jax.random.normal(key, dims, jnp.float32)
    if cuts:
        drawn = drawn * levels(key, dims, cuts, -0.22, 0.18)
    return jnp.clip(drawn, -limit, limit).astype(kind)


def setup_inputs(seed: int = 0) -> dict:
    seeds = jax.random.split(jax.random.key(seed), 13)
    return {
        "eta": normal_values(seeds[0], (NF, CELLS), 1.0, 6.0, ((1, 32),), jnp.float32),
        "forcing": normal_values(seeds[1], (NF, CELLS), 0.5, 3.0, ((1, 32),), jnp.float32),
        "couplings": jnp.clip(jnp.exp(math.log(0.3) - 2.7080503 * jax.random.uniform(seeds[2], (NB, CELLS), jnp.float32) ** levels(seeds[2], (NB, CELLS), ((1, 32),), -0.2, 0.2)), 0.02, 0.3),
        "neighbors": draw_neighbors(jax.random.fold_in(seeds[12], 71), 0),
        "halo_send": touch_ends(jax.random.randint(seeds[4], (N_GX * N_GY, 2 * HALO), 0, CELLS_DEV), jax.random.fold_in(seeds[4], 1), 0, CELLS_DEV - 1).astype(jnp.int32),
        "cycle_send": touch_ends(jax.random.randint(seeds[5], (N_GX * N_GY, BAND, CAP), 0, CELLS_DEV), jax.random.fold_in(seeds[5], 1), 0, CELLS_DEV - 1).astype(jnp.int32),
        "stencil": touch_ends(jax.random.randint(seeds[6], (NB, NLAT * NLON), 0, SLOTS), jax.random.fold_in(seeds[6], 1), 0, SLOTS - 1).astype(jnp.int32),
        "stencil_weights": draw_stencil_weights(jax.random.fold_in(seeds[12], 71), 0),
        "m_order": draw_m_order(jax.random.fold_in(seeds[12], 71), 0),
        "lat_weights": jnp.clip(jax.random.uniform(seeds[9], (NLAT,), jnp.float32, 0.5, 1.5), 0.5, 1.5),
        "love": jnp.clip(jnp.exp(jax.random.uniform(seeds[10], (DEG,), jnp.float32, math.log(0.1), math.log(2.0))), 0.1, 2.0),
        "legendre": draw_legendre(jax.random.fold_in(seeds[12], 71), 0),
    }


def wave_tables(m_order, points_count):
    points = jnp.arange(points_count, dtype=jnp.int32)
    phase = (points[:, None] * m_order[None, :].astype(jnp.int32)) % points_count
    angle = phase.astype(jnp.float32) * (2.0 * math.pi / points_count)
    return jnp.cos(angle), jnp.sin(angle)


def reference(eta, forcing, couplings, neighbors, halo_send, cycle_send, stencil, stencil_weights, m_order, lat_weights, love, legendre):
    partitions = N_GX * N_GY
    fields = eta.shape[0]
    rim_width = HALO
    slot_count = CAP
    points = CYCLES_DEV * NLON
    cells_now = eta.reshape(fields, partitions, CELLS_DEV)
    rim_index = jnp.broadcast_to(halo_send.reshape(1, partitions, 2 * rim_width), (fields, partitions, 2 * rim_width))
    rim_values = jnp.take_along_axis(cells_now, rim_index, axis=2)
    from_lower = jnp.roll(rim_values, 1, axis=1)[:, :, rim_width:]
    from_upper = jnp.roll(rim_values, -1, axis=1)[:, :, :rim_width]
    extended = jnp.concatenate([cells_now, from_lower, from_upper], axis=2)
    neighbor_index = neighbors.reshape(NB, partitions, CELLS_DEV)
    coupling = couplings.reshape(NB, partitions, CELLS_DEV)
    change = jnp.zeros(cells_now.shape, jnp.float32)
    for which in range(NB):
        values = jnp.take_along_axis(extended, jnp.broadcast_to(neighbor_index[which][None], cells_now.shape), axis=2)
        change = change + coupling[which][None] * (values - cells_now)
    stepped = cells_now + change + forcing.reshape(fields, partitions, CELLS_DEV)
    send_index = jnp.broadcast_to(cycle_send.reshape(1, partitions, BAND * slot_count), (fields, partitions, BAND * slot_count))
    outgoing = jnp.take_along_axis(stepped, send_index, axis=2).reshape(fields, partitions, BAND, slot_count)
    incoming = jnp.transpose(outgoing, (0, 2, 1, 3)).reshape(fields, BAND, partitions * slot_count)
    stencil_index = stencil.reshape(NB, partitions, points)
    stencil_wts = stencil_weights.reshape(NB, partitions, points)
    gridded = jnp.zeros((fields, partitions, points), jnp.float32)
    for which in range(NB):
        picked = jnp.take_along_axis(incoming, jnp.broadcast_to(stencil_index[which][None], (fields, partitions, points)), axis=2)
        gridded = gridded + stencil_wts[which][None] * picked
    cosines, sines = wave_tables(m_order, NLON)
    scale = NLON ** -0.5
    flat = gridded.reshape(fields * NLAT, NLON)
    cosine_part = jnp.dot(flat, cosines, precision=lax.Precision.HIGHEST, preferred_element_type=jnp.float32) * scale
    sine_part = jnp.dot(flat, sines, precision=lax.Precision.HIGHEST, preferred_element_type=jnp.float32) * scale
    fourier = jnp.stack([cosine_part, sine_part]).astype(jnp.bfloat16).reshape(2 * fields, NLAT, DEG)
    by_order = jnp.transpose(fourier, (2, 0, 1))

    def one_order(pair):
        spectra, legendre_rows = pair
        weighted = (spectra.astype(jnp.float32) * lat_weights[None, :]).astype(jnp.bfloat16)
        coefficients = jnp.dot(weighted, legendre_rows.T, preferred_element_type=jnp.float32)
        scaled = (coefficients * love[None, :]).astype(jnp.bfloat16)
        return jnp.dot(scaled, legendre_rows, preferred_element_type=jnp.float32).astype(jnp.bfloat16)

    synthesized = lax.map(one_order, (by_order, legendre))
    spectral = jnp.transpose(synthesized, (1, 2, 0)).astype(jnp.float32).reshape(2, fields * NLAT, DEG)
    returned_grid = jnp.dot(spectral[0], cosines.T, precision=lax.Precision.HIGHEST, preferred_element_type=jnp.float32)
    returned_grid = returned_grid + jnp.dot(spectral[1], sines.T, precision=lax.Precision.HIGHEST, preferred_element_type=jnp.float32)
    returned_grid = (returned_grid * scale).reshape(fields, partitions, points)

    def spread(index_rows, weight_rows, values):
        total = jnp.zeros((fields, partitions * slot_count), jnp.float32)
        for which in range(NB):
            total = total.at[:, index_rows[which]].add(weight_rows[which][None, :] * values)
        return total

    slot_sums = jax.vmap(spread, in_axes=(1, 1, 1))(stencil_index, stencil_wts, returned_grid)
    slot_sums = slot_sums.reshape(BAND, fields, partitions, slot_count)
    toward_cells = jnp.transpose(slot_sums, (2, 1, 0, 3)).reshape(partitions, fields, BAND * slot_count)

    def gather_home(index_row, values):
        return jnp.zeros((fields, CELLS_DEV), jnp.float32).at[:, index_row].add(values)

    loading = jax.vmap(gather_home)(cycle_send.reshape(partitions, BAND * slot_count), toward_cells)
    loading = jnp.transpose(loading, (1, 0, 2)).reshape(fields, partitions * CELLS_DEV)
    return stepped.reshape(fields, partitions * CELLS_DEV), loading
```

```python
import math

import jax
import jax.numpy as jnp
from jax import lax
from jax.sharding import PartitionSpec as P


from jax.experimental import pallas as pl
from jax.experimental.pallas import tpu as pltpu


def _block(total, cap=4096):
    size = math.gcd(total, cap)
    return size


def _vmem_limit(table_rows, copies):
    padded = -(-table_rows // 8) * 8 * 128 * 4
    return int(min(copies * padded + (16 << 20), 60 << 20))


def row_gather(index, table, terms=1, weights=None, unroll=8):
    rows, width = table.shape
    count = index.shape[0] // terms
    block = _block(count)

    def body(*refs):
        if weights is None:
            idx_ref, tab_hbm, out_ref, tab = refs
            w_ref = None
        else:
            idx_ref, w_ref, tab_hbm, out_ref, tab = refs

        @pl.when(pl.program_id(0) == 0)
        def _():
            pltpu.sync_copy(tab_hbm, tab)

        def step(g, carry):
            acc = None
            for k in range(terms):
                row = tab[pl.ds(idx_ref[terms * g + k], 1), :]
                if w_ref is not None:
                    row = w_ref[terms * g + k] * row
                acc = row if acc is None else acc + row
            out_ref[pl.ds(g, 1), :] = acc
            return carry

        lax.fori_loop(0, block, step, 0, unroll=unroll)

    smem = pl.BlockSpec((terms * block,), lambda i: (i,), memory_space=pltpu.SMEM)
    in_specs = [smem] + ([] if weights is None else [smem]) + [pl.BlockSpec(memory_space=pl.ANY)]
    operands = (index,) + (() if weights is None else (weights,)) + (table,)
    return pl.pallas_call(
        body,
        grid=(count // block,),
        in_specs=in_specs,
        out_specs=pl.BlockSpec((block, width), lambda i: (i, 0)),
        out_shape=jax.ShapeDtypeStruct((count, width), table.dtype),
        scratch_shapes=[pltpu.VMEM((rows, width), table.dtype)],
        compiler_params=pltpu.CompilerParams(
            dimension_semantics=("arbitrary",), vmem_limit_bytes=_vmem_limit(rows, 1)
        ),
    )(*operands)


def row_scatter(index, values, rows, terms=1, weights=None, unroll=8):
    count, width = values.shape
    block = _block(count)
    steps = count // block

    def body(*refs):
        if weights is None:
            idx_ref, val_ref, out_hbm, acc = refs
            w_ref = None
        else:
            idx_ref, w_ref, val_ref, out_hbm, acc = refs

        @pl.when(pl.program_id(0) == 0)
        def _():
            acc[...] = jnp.zeros(acc.shape, acc.dtype)

        def step(g, carry):
            row = val_ref[pl.ds(g, 1), :]
            for k in range(terms):
                t = idx_ref[terms * g + k]
                add = row if w_ref is None else w_ref[terms * g + k] * row
                acc[pl.ds(t, 1), :] += add
            return carry

        lax.fori_loop(0, block, step, 0, unroll=unroll)

        @pl.when(pl.program_id(0) == steps - 1)
        def _():
            pltpu.sync_copy(acc, out_hbm)

    smem = pl.BlockSpec((terms * block,), lambda i: (i,), memory_space=pltpu.SMEM)
    in_specs = [smem] + ([] if weights is None else [smem]) + [
        pl.BlockSpec((block, width), lambda i: (i, 0))
    ]
    operands = (index,) + (() if weights is None else (weights,)) + (values,)
    return pl.pallas_call(
        body,
        grid=(steps,),
        in_specs=in_specs,
        out_specs=pl.BlockSpec(memory_space=pl.ANY),
        out_shape=jax.ShapeDtypeStruct((rows, width), values.dtype),
        scratch_shapes=[pltpu.VMEM((rows, width), values.dtype)],
        compiler_params=pltpu.CompilerParams(
            dimension_semantics=("arbitrary",), vmem_limit_bytes=_vmem_limit(rows, 1)
        ),
    )(*operands)


def extended_2(cells, sides, width):
    for axis, dim in sides:
        count = lax.axis_size(axis)
        head = lax.slice_in_dim(cells, 0, width, axis=dim)
        tail = lax.slice_in_dim(cells, cells.shape[dim] - width, cells.shape[dim], axis=dim)
        cells = jnp.concatenate(
            [
                lax.ppermute(tail, axis, [(i, (i + 1) % count) for i in range(count)]),
                cells,
                lax.ppermute(head, axis, [((i + 1) % count, i) for i in range(count)]),
            ],
            axis=dim,
        )
    return cells


def wave_tables(m_order, points_count):
    points = jnp.arange(points_count, dtype=jnp.int32)
    phase = points[:, None] * m_order[None, :] % points_count
    angle = phase.astype(jnp.float32) * (2.0 * math.pi / points_count)
    return (jnp.cos(angle), jnp.sin(angle))


def on_device(
    eta,
    forcing,
    couplings,
    neighbors,
    halo_send,
    cycle_send,
    stencil,
    stencil_weights,
    m_order,
    lat_weights,
    love,
    legendre,
):
    fields, per_part = eta.shape
    terms = neighbors.shape[0]
    rim_width = halo_send.shape[1] // 2
    band_count = cycle_send.shape[1]
    slot_count = cycle_send.shape[2]
    orders_here = legendre.shape[0]
    lat_count = legendre.shape[2]
    size_x = lax.axis_size("gx")
    size_y = lax.axis_size("gy")
    partitions = size_x * size_y
    cycles_here = lat_count // partitions
    point_count = stencil.shape[1]
    lon_count = point_count // cycles_here
    degrees = m_order.shape[0]
    eta_rows = eta.T
    rim_values = jnp.take(eta, halo_send[0], axis=1)
    padded = extended_2(rim_values, ((("gx", "gy"), 1),), rim_width)
    extended = jnp.concatenate(
        [eta_rows, padded[:, :rim_width].T, padded[:, 3 * rim_width :].T], axis=0
    )
    picked_cells = row_gather(neighbors.reshape(-1), extended).reshape(terms, per_part, fields)
    change = jnp.zeros(eta_rows.shape, jnp.float32)
    for which in range(terms):
        change = change + couplings[which][:, None] * (picked_cells[which] - eta_rows)
    stepped_rows = eta_rows + change + forcing.T
    outgoing = row_gather(cycle_send[0].reshape(-1), stepped_rows).reshape(
        band_count, slot_count, fields
    )
    received = lax.all_to_all(outgoing, ("gx", "gy"), split_axis=0, concat_axis=0, tiled=True)
    incoming_rows = received.reshape(-1, fields)
    stencil_flat = stencil.T.reshape(-1)
    weights_flat = stencil_weights.T.reshape(-1)
    gridded_rows = row_gather(stencil_flat, incoming_rows, terms, weights_flat)
    gridded = gridded_rows.T
    cosines, sines = wave_tables(m_order, lon_count)
    scale = lon_count ** (-0.5)
    flat = gridded.reshape(fields * cycles_here, lon_count)
    cosine_part = (
        jnp.dot(flat, cosines, precision=lax.Precision.HIGHEST, preferred_element_type=jnp.float32)
        * scale
    )
    sine_part = (
        jnp.dot(flat, sines, precision=lax.Precision.HIGHEST, preferred_element_type=jnp.float32)
        * scale
    )
    fourier = jnp.stack([cosine_part, sine_part]).astype(jnp.bfloat16)
    fourier = fourier.reshape(2, fields, cycles_here, partitions, orders_here)
    fourier = jnp.transpose(fourier, (3, 4, 0, 1, 2)).reshape(partitions, -1)
    arrived = lax.all_to_all(
        lax.all_to_all(
            fourier.reshape(size_x, size_y, -1), "gx", split_axis=0, concat_axis=0, tiled=True
        ),
        "gy",
        split_axis=1,
        concat_axis=1,
        tiled=True,
    )
    arrived = arrived.reshape(partitions, orders_here, 2 * fields, cycles_here)
    spectra = jnp.transpose(arrived, (1, 2, 0, 3)).reshape(orders_here, 2 * fields, lat_count)
    weighted = (spectra.astype(jnp.float32) * lat_weights[None, None, :]).astype(jnp.bfloat16)
    coefficients = jnp.einsum(
        "jci,jli->jcl", weighted, legendre, preferred_element_type=jnp.float32
    )
    scaled = (coefficients * love[None, None, :]).astype(jnp.bfloat16)
    synthesized = jnp.einsum(
        "jcl,jli->jci", scaled, legendre, preferred_element_type=jnp.float32
    ).astype(jnp.bfloat16)
    leaving = synthesized.reshape(orders_here, 2 * fields, partitions, cycles_here)
    leaving = jnp.transpose(leaving, (2, 0, 1, 3)).reshape(partitions, -1)
    returned = lax.all_to_all(
        lax.all_to_all(
            leaving.reshape(size_x, size_y, -1), "gx", split_axis=0, concat_axis=0, tiled=True
        ),
        "gy",
        split_axis=1,
        concat_axis=1,
        tiled=True,
    )
    returned = returned.reshape(partitions, orders_here, 2, fields, cycles_here)
    spectral = (
        jnp.transpose(returned, (2, 3, 4, 0, 1))
        .reshape(2, fields * cycles_here, degrees)
        .astype(jnp.float32)
    )
    contract = (((1,), (1,)), ((), ()))
    returned_grid = lax.dot_general(
        spectral[0],
        cosines,
        contract,
        precision=lax.Precision.HIGHEST,
        preferred_element_type=jnp.float32,
    )
    returned_grid = returned_grid + lax.dot_general(
        spectral[1],
        sines,
        contract,
        precision=lax.Precision.HIGHEST,
        preferred_element_type=jnp.float32,
    )
    grid_rows = (returned_grid * scale).reshape(fields, -1).T
    slot_rows = row_scatter(stencil_flat, grid_rows, band_count * slot_count, terms, weights_flat)
    slot_rows = slot_rows.reshape(band_count, slot_count, fields)
    came_back = lax.all_to_all(slot_rows, ("gx", "gy"), split_axis=0, concat_axis=0, tiled=True)
    homeward = came_back.reshape(-1, fields)
    loading_rows = row_scatter(cycle_send[0].reshape(-1), homeward, per_part)
    return (stepped_rows.T, loading_rows.T)


def solution(mesh):
    placed = (
        P(None, ("gx", "gy")),
        P(None, ("gx", "gy")),
        P(None, ("gx", "gy")),
        P(None, ("gx", "gy")),
        P(("gx", "gy"), None),
        P(("gx", "gy"), None, None),
        P(None, ("gx", "gy")),
        P(None, ("gx", "gy")),
        P(),
        P(),
        P(),
        P(("gx", "gy"), None, None),
    )
    return jax.shard_map(
        on_device,
        mesh=mesh,
        in_specs=placed,
        out_specs=(P(None, ("gx", "gy")), P(None, ("gx", "gy"))),
        check_vma=False,
    )
```

```python
import math

import jax
import jax.numpy as jnp
from jax import lax
from jax.sharding import PartitionSpec as P


from jax.experimental import pallas as pl
from jax.experimental.pallas import tpu as pltpu


def _block(total, cap=4096):
    size = math.gcd(total, cap)
    return size


def _vmem_limit(table_rows, copies):
    padded = -(-table_rows // 8) * 8 * 128 * 4
    return int(min(copies * padded + (16 << 20), 60 << 20))


def row_gather(index, table, terms=1, weights=None, unroll=8):
    rows, width = table.shape
    count = index.shape[0] // terms
    block = _block(count)

    def body(*refs):
        if weights is None:
            idx_ref, tab_hbm, out_ref, tab = refs
            w_ref = None
        else:
            idx_ref, w_ref, tab_hbm, out_ref, tab = refs

        @pl.when(pl.program_id(0) == 0)
        def _():
            pltpu.sync_copy(tab_hbm, tab)

        def step(g, carry):
            acc = None
            for k in range(terms):
                row = tab[pl.ds(idx_ref[terms * g + k], 1), :]
                if w_ref is not None:
                    row = w_ref[terms * g + k] * row
                acc = row if acc is None else acc + row
            out_ref[pl.ds(g, 1), :] = acc
            return carry

        lax.fori_loop(0, block, step, 0, unroll=unroll)

    smem = pl.BlockSpec((terms * block,), lambda i: (i,), memory_space=pltpu.SMEM)
    in_specs = [smem] + ([] if weights is None else [smem]) + [pl.BlockSpec(memory_space=pl.ANY)]
    operands = (index,) + (() if weights is None else (weights,)) + (table,)
    return pl.pallas_call(
        body,
        grid=(count // block,),
        in_specs=in_specs,
        out_specs=pl.BlockSpec((block, width), lambda i: (i, 0)),
        out_shape=jax.ShapeDtypeStruct((count, width), table.dtype),
        scratch_shapes=[pltpu.VMEM((rows, width), table.dtype)],
        compiler_params=pltpu.CompilerParams(
            dimension_semantics=("arbitrary",), vmem_limit_bytes=_vmem_limit(rows, 1)
        ),
    )(*operands)


def row_scatter(index, values, rows, terms=1, weights=None, unroll=8):
    count, width = values.shape
    block = _block(count)
    steps = count // block
    copies = 6 if terms == 3 else 4
    lanes = copies // terms if copies % terms == 0 else 1
    copies = lanes * terms
    chunk = math.gcd(rows, 256)

    def body(*refs):
        if weights is None:
            idx_ref, val_ref, out_hbm = refs[:3]
            w_ref = None
            accs = refs[3:]
        else:
            idx_ref, w_ref, val_ref, out_hbm = refs[:4]
            accs = refs[4:]

        @pl.when(pl.program_id(0) == 0)
        def _():
            def clear(c, carry):
                for acc in accs:
                    acc[pl.ds(c * chunk, chunk), :] = jnp.zeros((chunk, width), acc.dtype)
                return carry

            lax.fori_loop(0, rows // chunk, clear, 0)

        def step(h, carry):
            for lane in range(lanes):
                g = h * lanes + lane
                row = val_ref[pl.ds(g, 1), :]
                for k in range(terms):
                    t = idx_ref[terms * g + k]
                    add = row if w_ref is None else w_ref[terms * g + k] * row
                    acc = accs[lane * terms + k]
                    acc[pl.ds(t, 1), :] += add
            return carry

        lax.fori_loop(0, block // lanes, step, 0, unroll=unroll)

        @pl.when(pl.program_id(0) == steps - 1)
        def _():
            def fold(c, carry):
                part = pl.ds(c * chunk, chunk)
                total = accs[0][part, :]
                for acc in accs[1:]:
                    total = total + acc[part, :]
                accs[0][part, :] = total
                return carry

            lax.fori_loop(0, rows // chunk, fold, 0)
            pltpu.sync_copy(accs[0], out_hbm)

    smem = pl.BlockSpec((terms * block,), lambda i: (i,), memory_space=pltpu.SMEM)
    in_specs = [smem] + ([] if weights is None else [smem]) + [
        pl.BlockSpec((block, width), lambda i: (i, 0))
    ]
    operands = (index,) + (() if weights is None else (weights,)) + (values,)
    return pl.pallas_call(
        body,
        grid=(steps,),
        in_specs=in_specs,
        out_specs=pl.BlockSpec(memory_space=pl.ANY),
        out_shape=jax.ShapeDtypeStruct((rows, width), values.dtype),
        scratch_shapes=[pltpu.VMEM((rows, width), values.dtype) for _ in range(copies)],
        compiler_params=pltpu.CompilerParams(
            dimension_semantics=("arbitrary",), vmem_limit_bytes=_vmem_limit(rows, copies)
        ),
    )(*operands)


def extended_2(cells, sides, width):
    for axis, dim in sides:
        count = lax.axis_size(axis)
        head = lax.slice_in_dim(cells, 0, width, axis=dim)
        tail = lax.slice_in_dim(cells, cells.shape[dim] - width, cells.shape[dim], axis=dim)
        cells = jnp.concatenate(
            [
                lax.ppermute(tail, axis, [(i, (i + 1) % count) for i in range(count)]),
                cells,
                lax.ppermute(head, axis, [((i + 1) % count, i) for i in range(count)]),
            ],
            axis=dim,
        )
    return cells


def wave_tables(m_order, points_count):
    points = jnp.arange(points_count, dtype=jnp.int32)
    phase = points[:, None] * m_order[None, :] % points_count
    angle = phase.astype(jnp.float32) * (2.0 * math.pi / points_count)
    return (jnp.cos(angle), jnp.sin(angle))


def on_device(
    eta,
    forcing,
    couplings,
    neighbors,
    halo_send,
    cycle_send,
    stencil,
    stencil_weights,
    m_order,
    lat_weights,
    love,
    legendre,
):
    fields, per_part = eta.shape
    terms = neighbors.shape[0]
    rim_width = halo_send.shape[1] // 2
    band_count = cycle_send.shape[1]
    slot_count = cycle_send.shape[2]
    orders_here = legendre.shape[0]
    lat_count = legendre.shape[2]
    size_x = lax.axis_size("gx")
    size_y = lax.axis_size("gy")
    partitions = size_x * size_y
    cycles_here = lat_count // partitions
    point_count = stencil.shape[1]
    lon_count = point_count // cycles_here
    degrees = m_order.shape[0]
    eta_rows = eta.T
    rim_values = jnp.take(eta, halo_send[0], axis=1)
    padded = extended_2(rim_values, ((("gx", "gy"), 1),), rim_width)
    extended = jnp.concatenate(
        [eta_rows, padded[:, :rim_width].T, padded[:, 3 * rim_width :].T], axis=0
    )
    picked_cells = row_gather(neighbors.reshape(-1), extended).reshape(terms, per_part, fields)
    change = jnp.zeros(eta_rows.shape, jnp.float32)
    for which in range(terms):
        change = change + couplings[which][:, None] * (picked_cells[which] - eta_rows)
    stepped_rows = eta_rows + change + forcing.T
    outgoing = row_gather(cycle_send[0].reshape(-1), stepped_rows).reshape(
        band_count, slot_count, fields
    )
    received = lax.all_to_all(outgoing, ("gx", "gy"), split_axis=0, concat_axis=0, tiled=True)
    incoming_rows = received.reshape(-1, fields)
    stencil_flat = stencil.T.reshape(-1)
    weights_flat = stencil_weights.T.reshape(-1)
    gridded_rows = row_gather(stencil_flat, incoming_rows, terms, weights_flat)
    gridded = gridded_rows.T
    cosines, sines = wave_tables(m_order, lon_count)
    scale = lon_count ** (-0.5)
    flat = gridded.reshape(fields * cycles_here, lon_count)
    cosine_part = (
        jnp.dot(flat, cosines, precision=lax.Precision.HIGH, preferred_element_type=jnp.float32)
        * scale
    )
    sine_part = (
        jnp.dot(flat, sines, precision=lax.Precision.HIGH, preferred_element_type=jnp.float32)
        * scale
    )
    fourier = jnp.stack([cosine_part, sine_part]).astype(jnp.bfloat16)
    fourier = fourier.reshape(2, fields, cycles_here, partitions, orders_here)
    fourier = jnp.transpose(fourier, (3, 4, 0, 1, 2)).reshape(partitions, -1)
    arrived = lax.all_to_all(
        lax.all_to_all(
            fourier.reshape(size_x, size_y, -1), "gx", split_axis=0, concat_axis=0, tiled=True
        ),
        "gy",
        split_axis=1,
        concat_axis=1,
        tiled=True,
    )
    arrived = arrived.reshape(partitions, orders_here, 2 * fields, cycles_here)
    spectra = jnp.transpose(arrived, (1, 2, 0, 3)).reshape(orders_here, 2 * fields, lat_count)
    weighted = (spectra.astype(jnp.float32) * lat_weights[None, None, :]).astype(jnp.bfloat16)
    coefficients = jnp.einsum(
        "jci,jli->jcl", weighted, legendre, preferred_element_type=jnp.float32
    )
    scaled = (coefficients * love[None, None, :]).astype(jnp.bfloat16)
    synthesized = jnp.einsum(
        "jcl,jli->jci", scaled, legendre, preferred_element_type=jnp.float32
    ).astype(jnp.bfloat16)
    leaving = synthesized.reshape(orders_here, 2 * fields, partitions, cycles_here)
    leaving = jnp.transpose(leaving, (2, 0, 1, 3)).reshape(partitions, -1)
    returned = lax.all_to_all(
        lax.all_to_all(
            leaving.reshape(size_x, size_y, -1), "gx", split_axis=0, concat_axis=0, tiled=True
        ),
        "gy",
        split_axis=1,
        concat_axis=1,
        tiled=True,
    )
    returned = returned.reshape(partitions, orders_here, 2, fields, cycles_here)
    spectral = jnp.transpose(returned, (2, 3, 4, 0, 1)).reshape(2, fields * cycles_here, degrees)
    contract = (((1,), (1,)), ((), ()))
    returned_grid = None
    for part, table in ((0, cosines), (1, sines)):
        high = table.astype(jnp.bfloat16)
        low = (table - high.astype(jnp.float32)).astype(jnp.bfloat16)
        for piece in (high, low):
            term = lax.dot_general(
                spectral[part], piece, contract, preferred_element_type=jnp.float32
            )
            returned_grid = term if returned_grid is None else returned_grid + term
    grid_rows = (returned_grid * scale).reshape(fields, -1).T
    slot_rows = row_scatter(stencil_flat, grid_rows, band_count * slot_count, terms, weights_flat)
    slot_rows = slot_rows.reshape(band_count, slot_count, fields)
    came_back = lax.all_to_all(slot_rows, ("gx", "gy"), split_axis=0, concat_axis=0, tiled=True)
    homeward = came_back.reshape(-1, fields)
    loading_rows = row_scatter(cycle_send[0].reshape(-1), homeward, per_part)
    return (stepped_rows.T, loading_rows.T)


def solution(mesh):
    placed = (
        P(None, ("gx", "gy")),
        P(None, ("gx", "gy")),
        P(None, ("gx", "gy")),
        P(None, ("gx", "gy")),
        P(("gx", "gy"), None),
        P(("gx", "gy"), None, None),
        P(None, ("gx", "gy")),
        P(None, ("gx", "gy")),
        P(),
        P(),
        P(),
        P(("gx", "gy"), None, None),
    )
    return jax.shard_map(
        on_device,
        mesh=mesh,
        in_specs=placed,
        out_specs=(P(None, ("gx", "gy")), P(None, ("gx", "gy"))),
        check_vma=False,
    )
```

```python
import math

import jax
import jax.numpy as jnp
from jax import lax
from jax.sharding import PartitionSpec as P


from jax.experimental import pallas as pl
from jax.experimental.pallas import tpu as pltpu


def _block(total, cap=4096):
    size = math.gcd(total, cap)
    return size


def _vmem_limit(table_rows, copies):
    padded = -(-table_rows // 8) * 8 * 128 * 4
    return int(min(copies * padded + (16 << 20), 60 << 20))


def row_gather(index, table, terms=1, weights=None, unroll=8):
    rows, width = table.shape
    count = index.shape[0] // terms
    block = _block(count)

    def body(*refs):
        if weights is None:
            idx_ref, tab_hbm, out_ref, tab = refs
            w_ref = None
        else:
            idx_ref, w_ref, tab_hbm, out_ref, tab = refs

        @pl.when(pl.program_id(0) == 0)
        def _():
            pltpu.sync_copy(tab_hbm, tab)

        def step(g, carry):
            acc = None
            for k in range(terms):
                row = tab[pl.ds(idx_ref[terms * g + k], 1), :]
                if w_ref is not None:
                    row = w_ref[terms * g + k] * row
                acc = row if acc is None else acc + row
            out_ref[pl.ds(g, 1), :] = acc
            return carry

        lax.fori_loop(0, block, step, 0, unroll=unroll)

    smem = pl.BlockSpec((terms * block,), lambda i: (i,), memory_space=pltpu.SMEM)
    in_specs = [smem] + ([] if weights is None else [smem]) + [pl.BlockSpec(memory_space=pl.ANY)]
    operands = (index,) + (() if weights is None else (weights,)) + (table,)
    return pl.pallas_call(
        body,
        grid=(count // block,),
        in_specs=in_specs,
        out_specs=pl.BlockSpec((block, width), lambda i: (i, 0)),
        out_shape=jax.ShapeDtypeStruct((count, width), table.dtype),
        scratch_shapes=[pltpu.VMEM((rows, width), table.dtype)],
        compiler_params=pltpu.CompilerParams(
            dimension_semantics=("arbitrary",), vmem_limit_bytes=_vmem_limit(rows, 1)
        ),
    )(*operands)


def row_scatter(index, values, rows, terms=1, weights=None, unroll=8):
    count, width = values.shape
    block = _block(count)
    steps = count // block
    copies = 6 if terms == 3 else 4
    lanes = copies // terms if copies % terms == 0 else 1
    copies = lanes * terms
    chunk = math.gcd(rows, 256)

    def body(*refs):
        if weights is None:
            idx_ref, val_ref, out_hbm = refs[:3]
            w_ref = None
            accs = refs[3:]
        else:
            idx_ref, w_ref, val_ref, out_hbm = refs[:4]
            accs = refs[4:]

        @pl.when(pl.program_id(0) == 0)
        def _():
            def clear(c, carry):
                for acc in accs:
                    acc[pl.ds(c * chunk, chunk), :] = jnp.zeros((chunk, width), acc.dtype)
                return carry

            lax.fori_loop(0, rows // chunk, clear, 0)

        def step(h, carry):
            for lane in range(lanes):
                g = h * lanes + lane
                row = val_ref[pl.ds(g, 1), :]
                for k in range(terms):
                    t = idx_ref[terms * g + k]
                    add = row if w_ref is None else w_ref[terms * g + k] * row
                    acc = accs[lane * terms + k]
                    acc[pl.ds(t, 1), :] += add
            return carry

        lax.fori_loop(0, block // lanes, step, 0, unroll=unroll)

        @pl.when(pl.program_id(0) == steps - 1)
        def _():
            def fold(c, carry):
                part = pl.ds(c * chunk, chunk)
                total = accs[0][part, :]
                for acc in accs[1:]:
                    total = total + acc[part, :]
                accs[0][part, :] = total
                return carry

            lax.fori_loop(0, rows // chunk, fold, 0)
            pltpu.sync_copy(accs[0], out_hbm)

    smem = pl.BlockSpec((terms * block,), lambda i: (i,), memory_space=pltpu.SMEM)
    in_specs = [smem] + ([] if weights is None else [smem]) + [
        pl.BlockSpec((block, width), lambda i: (i, 0))
    ]
    operands = (index,) + (() if weights is None else (weights,)) + (values,)
    return pl.pallas_call(
        body,
        grid=(steps,),
        in_specs=in_specs,
        out_specs=pl.BlockSpec(memory_space=pl.ANY),
        out_shape=jax.ShapeDtypeStruct((rows, width), values.dtype),
        scratch_shapes=[pltpu.VMEM((rows, width), values.dtype) for _ in range(copies)],
        compiler_params=pltpu.CompilerParams(
            dimension_semantics=("arbitrary",), vmem_limit_bytes=_vmem_limit(rows, copies)
        ),
    )(*operands)


def extended_2(cells, sides, width):
    for axis, dim in sides:
        count = lax.axis_size(axis)
        head = lax.slice_in_dim(cells, 0, width, axis=dim)
        tail = lax.slice_in_dim(cells, cells.shape[dim] - width, cells.shape[dim], axis=dim)
        cells = jnp.concatenate(
            [
                lax.ppermute(tail, axis, [(i, (i + 1) % count) for i in range(count)]),
                cells,
                lax.ppermute(head, axis, [((i + 1) % count, i) for i in range(count)]),
            ],
            axis=dim,
        )
    return cells


def split_bf16(values):
    high = values.astype(jnp.bfloat16)
    low = (values - high.astype(jnp.float32)).astype(jnp.bfloat16)
    return high, low


def wave_tables(m_order, points_count):
    points = jnp.arange(points_count, dtype=jnp.int32)
    phase = points[:, None] * m_order[None, :] % points_count
    angle = phase.astype(jnp.float32) * (2.0 * math.pi / points_count)
    return (jnp.cos(angle), jnp.sin(angle))


def on_device(
    eta,
    forcing,
    couplings,
    neighbors,
    halo_send,
    cycle_send,
    stencil,
    stencil_weights,
    m_order,
    lat_weights,
    love,
    legendre,
):
    fields, per_part = eta.shape
    terms = neighbors.shape[0]
    rim_width = halo_send.shape[1] // 2
    band_count = cycle_send.shape[1]
    slot_count = cycle_send.shape[2]
    orders_here = legendre.shape[0]
    lat_count = legendre.shape[2]
    size_x = lax.axis_size("gx")
    size_y = lax.axis_size("gy")
    partitions = size_x * size_y
    cycles_here = lat_count // partitions
    point_count = stencil.shape[1]
    lon_count = point_count // cycles_here
    degrees = m_order.shape[0]
    eta_rows = eta.T
    rim_values = jnp.take(eta, halo_send[0], axis=1)
    padded = extended_2(rim_values, ((("gx", "gy"), 1),), rim_width)
    extended = jnp.concatenate(
        [eta_rows, padded[:, :rim_width].T, padded[:, 3 * rim_width :].T], axis=0
    )
    picked_cells = row_gather(neighbors.reshape(-1), extended).reshape(terms, per_part, fields)
    change = jnp.zeros(eta_rows.shape, jnp.float32)
    for which in range(terms):
        change = change + couplings[which][:, None] * (picked_cells[which] - eta_rows)
    stepped_rows = eta_rows + change + forcing.T
    outgoing = row_gather(cycle_send[0].reshape(-1), stepped_rows).reshape(
        band_count, slot_count, fields
    )
    received = lax.all_to_all(outgoing, ("gx", "gy"), split_axis=0, concat_axis=0, tiled=True)
    incoming_rows = received.reshape(-1, fields)
    stencil_flat = stencil.T.reshape(-1)
    weights_flat = stencil_weights.T.reshape(-1)
    gridded_rows = row_gather(stencil_flat, incoming_rows, terms, weights_flat)
    gridded = gridded_rows.T
    cosines, sines = wave_tables(m_order, lon_count)
    table_high, table_low = split_bf16(jnp.concatenate([cosines, sines], axis=1))
    table_high, table_low = lax.optimization_barrier((table_high, table_low))
    scale = lon_count ** (-0.5)
    flat = gridded.reshape(fields * cycles_here, lon_count)
    flat_high, flat_low = split_bf16(flat)
    forward = None
    for left, right in ((flat_high, table_high), (flat_low, table_high), (flat_high, table_low)):
        term = jnp.dot(left, right, preferred_element_type=jnp.float32)
        forward = term if forward is None else forward + term
    fourier = (forward * scale).astype(jnp.bfloat16)
    fourier = fourier.reshape(fields, cycles_here, 2, partitions, orders_here)
    fourier = jnp.transpose(fourier, (3, 4, 2, 0, 1)).reshape(partitions, -1)
    arrived = lax.all_to_all(
        lax.all_to_all(
            fourier.reshape(size_x, size_y, -1), "gx", split_axis=0, concat_axis=0, tiled=True
        ),
        "gy",
        split_axis=1,
        concat_axis=1,
        tiled=True,
    )
    arrived = arrived.reshape(partitions, orders_here, 2 * fields, cycles_here)
    spectra = jnp.transpose(arrived, (1, 2, 0, 3)).reshape(orders_here, 2 * fields, lat_count)
    weighted = (spectra.astype(jnp.float32) * lat_weights[None, None, :]).astype(jnp.bfloat16)
    coefficients = jnp.einsum(
        "jci,jli->jcl", weighted, legendre, preferred_element_type=jnp.float32
    )
    scaled = (coefficients * love[None, None, :]).astype(jnp.bfloat16)
    synthesized = jnp.einsum(
        "jcl,jli->jci", scaled, legendre, preferred_element_type=jnp.float32
    ).astype(jnp.bfloat16)
    leaving = synthesized.reshape(orders_here, 2 * fields, partitions, cycles_here)
    leaving = jnp.transpose(leaving, (2, 0, 1, 3)).reshape(partitions, -1)
    returned = lax.all_to_all(
        lax.all_to_all(
            leaving.reshape(size_x, size_y, -1), "gx", split_axis=0, concat_axis=0, tiled=True
        ),
        "gy",
        split_axis=1,
        concat_axis=1,
        tiled=True,
    )
    returned = returned.reshape(partitions, orders_here, 2, fields, cycles_here)
    spectral = jnp.transpose(returned, (3, 4, 2, 0, 1)).reshape(fields * cycles_here, 2 * degrees)
    contract = (((1,), (1,)), ((), ()))
    returned_grid = None
    for piece in (table_high, table_low):
        term = lax.dot_general(spectral, piece, contract, preferred_element_type=jnp.float32)
        returned_grid = term if returned_grid is None else returned_grid + term
    grid_rows = (returned_grid * scale).reshape(fields, -1).T
    slot_rows = row_scatter(stencil_flat, grid_rows, band_count * slot_count, terms, weights_flat)
    slot_rows = slot_rows.reshape(band_count, slot_count, fields)
    came_back = lax.all_to_all(slot_rows, ("gx", "gy"), split_axis=0, concat_axis=0, tiled=True)
    homeward = came_back.reshape(-1, fields)
    loading_rows = row_scatter(cycle_send[0].reshape(-1), homeward, per_part)
    return (stepped_rows.T, loading_rows.T)


def solution(mesh):
    placed = (
        P(None, ("gx", "gy")),
        P(None, ("gx", "gy")),
        P(None, ("gx", "gy")),
        P(None, ("gx", "gy")),
        P(("gx", "gy"), None),
        P(("gx", "gy"), None, None),
        P(None, ("gx", "gy")),
        P(None, ("gx", "gy")),
        P(),
        P(),
        P(),
        P(("gx", "gy"), None, None),
    )
    return jax.shard_map(
        on_device,
        mesh=mesh,
        in_specs=placed,
        out_specs=(P(None, ("gx", "gy")), P(None, ("gx", "gy"))),
        check_vma=False,
    )
```

```python
import math

import jax
import jax.numpy as jnp
from jax import lax
from jax.sharding import PartitionSpec as P


from jax.experimental import pallas as pl
from jax.experimental.pallas import tpu as pltpu


def _block(total, cap=4096):
    size = math.gcd(total, cap)
    return size


def _vmem_limit(table_rows, copies):
    padded = -(-table_rows // 8) * 8 * 128 * 4
    return int(min(copies * padded + (16 << 20), 60 << 20))


def row_gather(indices, table, weights=None, unroll=8):
    rows, width = table.shape
    terms = len(indices)
    count = indices[0].shape[0]
    block = _block(count)
    scales = [] if weights is None else list(weights)

    def body(*refs):
        idx_refs = refs[:terms]
        w_refs = refs[terms : terms + len(scales)]
        tab_hbm, out_ref, tab = refs[terms + len(scales) :]

        @pl.when(pl.program_id(0) == 0)
        def _():
            pltpu.sync_copy(tab_hbm, tab)

        def step(g, carry):
            acc = None
            for k in range(terms):
                row = tab[pl.ds(idx_refs[k][g], 1), :]
                if w_refs:
                    row = w_refs[k][g] * row
                acc = row if acc is None else acc + row
            out_ref[pl.ds(g, 1), :] = acc
            return carry

        lax.fori_loop(0, block, step, 0, unroll=unroll)

    smem = pl.BlockSpec((block,), lambda i: (i,), memory_space=pltpu.SMEM)
    return pl.pallas_call(
        body,
        grid=(count // block,),
        in_specs=[smem] * (terms + len(scales)) + [pl.BlockSpec(memory_space=pl.ANY)],
        out_specs=pl.BlockSpec((block, width), lambda i: (i, 0)),
        out_shape=jax.ShapeDtypeStruct((count, width), table.dtype),
        scratch_shapes=[pltpu.VMEM((rows, width), table.dtype)],
        compiler_params=pltpu.CompilerParams(
            dimension_semantics=("arbitrary",), vmem_limit_bytes=_vmem_limit(rows, 1)
        ),
    )(*indices, *scales, table)


def row_scatter(indices, values, rows, weights=None, unroll=8):
    count, width = values.shape
    terms = len(indices)
    block = _block(count)
    steps = count // block
    scales = [] if weights is None else list(weights)
    copies = 6 if terms == 3 else 4
    lanes = copies // terms if copies % terms == 0 else 1
    copies = lanes * terms
    chunk = math.gcd(rows, 256)

    def body(*refs):
        idx_refs = refs[:terms]
        w_refs = refs[terms : terms + len(scales)]
        val_ref, out_hbm = refs[terms + len(scales) : terms + len(scales) + 2]
        accs = refs[terms + len(scales) + 2 :]

        @pl.when(pl.program_id(0) == 0)
        def _():
            def clear(c, carry):
                for acc in accs:
                    acc[pl.ds(c * chunk, chunk), :] = jnp.zeros((chunk, width), acc.dtype)
                return carry

            lax.fori_loop(0, rows // chunk, clear, 0)

        def step(h, carry):
            for lane in range(lanes):
                g = h * lanes + lane
                row = val_ref[pl.ds(g, 1), :]
                for k in range(terms):
                    add = w_refs[k][g] * row if w_refs else row
                    acc = accs[lane * terms + k]
                    acc[pl.ds(idx_refs[k][g], 1), :] += add
            return carry

        lax.fori_loop(0, block // lanes, step, 0, unroll=unroll)

        @pl.when(pl.program_id(0) == steps - 1)
        def _():
            def fold(c, carry):
                part = pl.ds(c * chunk, chunk)
                total = accs[0][part, :]
                for acc in accs[1:]:
                    total = total + acc[part, :]
                accs[0][part, :] = total
                return carry

            lax.fori_loop(0, rows // chunk, fold, 0)
            pltpu.sync_copy(accs[0], out_hbm)

    smem = pl.BlockSpec((block,), lambda i: (i,), memory_space=pltpu.SMEM)
    return pl.pallas_call(
        body,
        grid=(steps,),
        in_specs=[smem] * (terms + len(scales)) + [pl.BlockSpec((block, width), lambda i: (i, 0))],
        out_specs=pl.BlockSpec(memory_space=pl.ANY),
        out_shape=jax.ShapeDtypeStruct((rows, width), values.dtype),
        scratch_shapes=[pltpu.VMEM((rows, width), values.dtype) for _ in range(copies)],
        compiler_params=pltpu.CompilerParams(
            dimension_semantics=("arbitrary",), vmem_limit_bytes=_vmem_limit(rows, copies)
        ),
    )(*indices, *scales, values)


def extended_2(cells, sides, width):
    for axis, dim in sides:
        count = lax.axis_size(axis)
        head = lax.slice_in_dim(cells, 0, width, axis=dim)
        tail = lax.slice_in_dim(cells, cells.shape[dim] - width, cells.shape[dim], axis=dim)
        cells = jnp.concatenate(
            [
                lax.ppermute(tail, axis, [(i, (i + 1) % count) for i in range(count)]),
                cells,
                lax.ppermute(head, axis, [((i + 1) % count, i) for i in range(count)]),
            ],
            axis=dim,
        )
    return cells


def split_bf16(values):
    kept = lax.reduce_precision(values, exponent_bits=8, mantissa_bits=7)
    return kept.astype(jnp.bfloat16), (values - kept).astype(jnp.bfloat16)


def wave_tables(m_order, points_count):
    points = jnp.arange(points_count, dtype=jnp.int32)
    phase = points[:, None] * m_order[None, :] % points_count
    angle = phase.astype(jnp.float32) * (2.0 * math.pi / points_count)
    return (jnp.cos(angle), jnp.sin(angle))


def on_device(
    eta,
    forcing,
    couplings,
    neighbors,
    halo_send,
    cycle_send,
    stencil,
    stencil_weights,
    m_order,
    lat_weights,
    love,
    legendre,
):
    fields, per_part = eta.shape
    terms = neighbors.shape[0]
    rim_width = halo_send.shape[1] // 2
    band_count = cycle_send.shape[1]
    slot_count = cycle_send.shape[2]
    orders_here = legendre.shape[0]
    lat_count = legendre.shape[2]
    size_x = lax.axis_size("gx")
    size_y = lax.axis_size("gy")
    partitions = size_x * size_y
    cycles_here = lat_count // partitions
    point_count = stencil.shape[1]
    lon_count = point_count // cycles_here
    degrees = m_order.shape[0]
    eta_rows = eta.T
    rim_values = jnp.take(eta, halo_send[0], axis=1)
    padded = extended_2(rim_values, ((("gx", "gy"), 1),), rim_width)
    extended = jnp.concatenate(
        [eta_rows, padded[:, :rim_width].T, padded[:, 3 * rim_width :].T], axis=0
    )
    picked_cells = row_gather([neighbors.reshape(-1)], extended).reshape(terms, per_part, fields)
    change = jnp.zeros(eta_rows.shape, jnp.float32)
    for which in range(terms):
        change = change + couplings[which][:, None] * (picked_cells[which] - eta_rows)
    stepped_rows = eta_rows + change + forcing.T
    outgoing = row_gather([cycle_send[0].reshape(-1)], stepped_rows).reshape(
        band_count, slot_count, fields
    )
    received = lax.all_to_all(outgoing, ("gx", "gy"), split_axis=0, concat_axis=0, tiled=True)
    incoming_rows = received.reshape(-1, fields)
    stencil_rows = [stencil[which] for which in range(terms)]
    weight_rows = [stencil_weights[which] for which in range(terms)]
    gridded_rows = row_gather(stencil_rows, incoming_rows, weight_rows)
    gridded = gridded_rows.T
    cosines, sines = wave_tables(m_order, lon_count)
    table_high, table_low = split_bf16(jnp.concatenate([cosines, sines], axis=1))
    table_high, table_low = lax.optimization_barrier((table_high, table_low))
    scale = lon_count ** (-0.5)
    flat = gridded.reshape(fields * cycles_here, lon_count)
    flat_high, flat_low = split_bf16(flat)
    forward = None
    for left, right in ((flat_high, table_high), (flat_low, table_high), (flat_high, table_low)):
        term = jnp.dot(left, right, preferred_element_type=jnp.float32)
        forward = term if forward is None else forward + term
    fourier = (forward * scale).astype(jnp.bfloat16)
    fourier = fourier.reshape(fields, cycles_here, 2, partitions, orders_here)
    fourier = jnp.transpose(fourier, (3, 4, 2, 0, 1)).reshape(partitions, -1)
    arrived = lax.all_to_all(fourier, ("gx", "gy"), split_axis=0, concat_axis=0, tiled=True)
    arrived = arrived.reshape(partitions, orders_here, 2 * fields, cycles_here)
    spectra = jnp.transpose(arrived, (1, 2, 0, 3)).reshape(orders_here, 2 * fields, lat_count)
    weighted = (spectra.astype(jnp.float32) * lat_weights[None, None, :]).astype(jnp.bfloat16)
    coefficients = jnp.einsum(
        "jci,jli->jcl", weighted, legendre, preferred_element_type=jnp.float32
    )
    scaled = (coefficients * love[None, None, :]).astype(jnp.bfloat16)
    synthesized = jnp.einsum(
        "jcl,jli->jci", scaled, legendre, preferred_element_type=jnp.float32
    ).astype(jnp.bfloat16)
    leaving = synthesized.reshape(orders_here, 2 * fields, partitions, cycles_here)
    leaving = jnp.transpose(leaving, (2, 0, 1, 3)).reshape(partitions, -1)
    returned = lax.all_to_all(leaving, ("gx", "gy"), split_axis=0, concat_axis=0, tiled=True)
    returned = returned.reshape(partitions, orders_here, 2, fields, cycles_here)
    spectral = jnp.transpose(returned, (3, 4, 2, 0, 1)).reshape(fields * cycles_here, 2 * degrees)
    contract = (((1,), (1,)), ((), ()))
    returned_grid = None
    for piece in (table_high, table_low):
        term = lax.dot_general(spectral, piece, contract, preferred_element_type=jnp.float32)
        returned_grid = term if returned_grid is None else returned_grid + term
    grid_rows = (returned_grid * scale).reshape(fields, -1).T
    slot_rows = row_scatter(stencil_rows, grid_rows, band_count * slot_count, weight_rows)
    slot_rows = slot_rows.reshape(band_count, slot_count, fields)
    came_back = lax.all_to_all(slot_rows, ("gx", "gy"), split_axis=0, concat_axis=0, tiled=True)
    homeward = came_back.reshape(-1, fields)
    loading_rows = row_scatter([cycle_send[0].reshape(-1)], homeward, per_part)
    return (stepped_rows.T, loading_rows.T)


def solution(mesh):
    placed = (
        P(None, ("gx", "gy")),
        P(None, ("gx", "gy")),
        P(None, ("gx", "gy")),
        P(None, ("gx", "gy")),
        P(("gx", "gy"), None),
        P(("gx", "gy"), None, None),
        P(None, ("gx", "gy")),
        P(None, ("gx", "gy")),
        P(),
        P(),
        P(),
        P(("gx", "gy"), None, None),
    )
    return jax.shard_map(
        on_device,
        mesh=mesh,
        in_specs=placed,
        out_specs=(P(None, ("gx", "gy")), P(None, ("gx", "gy"))),
        check_vma=False,
    )
```

```python
import math

import jax
import jax.numpy as jnp
from jax import lax
from jax.sharding import PartitionSpec as P


from jax.experimental import pallas as pl
from jax.experimental.pallas import tpu as pltpu


def _block(total, cap=4096):
    size = math.gcd(total, cap)
    return size


def _vmem_limit(table_rows, copies):
    padded = -(-table_rows // 8) * 8 * 128 * 4
    return int(min(copies * padded + (16 << 20), 60 << 20))


def row_gather(indices, table, weights=None, unroll=16):
    rows, width = table.shape
    terms = len(indices)
    count = indices[0].shape[0]
    block = _block(count)
    scales = [] if weights is None else list(weights)

    def body(*refs):
        idx_refs = refs[:terms]
        w_refs = refs[terms : terms + len(scales)]
        tab_hbm, out_ref, tab = refs[terms + len(scales) :]

        @pl.when(pl.program_id(0) == 0)
        def _():
            pltpu.sync_copy(tab_hbm, tab)

        def step(g, carry):
            acc = None
            for k in range(terms):
                row = tab[pl.ds(idx_refs[k][g], 1), :]
                if w_refs:
                    row = w_refs[k][g] * row
                acc = row if acc is None else acc + row
            out_ref[pl.ds(g, 1), :] = acc
            return carry

        lax.fori_loop(0, block, step, 0, unroll=unroll)

    smem = pl.BlockSpec((block,), lambda i: (i,), memory_space=pltpu.SMEM)
    return pl.pallas_call(
        body,
        grid=(count // block,),
        in_specs=[smem] * (terms + len(scales)) + [pl.BlockSpec(memory_space=pl.ANY)],
        out_specs=pl.BlockSpec((block, width), lambda i: (i, 0)),
        out_shape=jax.ShapeDtypeStruct((count, width), table.dtype),
        scratch_shapes=[pltpu.VMEM((rows, width), table.dtype)],
        compiler_params=pltpu.CompilerParams(
            dimension_semantics=("arbitrary",), vmem_limit_bytes=_vmem_limit(rows, 1)
        ),
    )(*indices, *scales, table)


def row_scatter(indices, values, rows, weights=None, unroll=16):
    count, width = values.shape
    terms = len(indices)
    block = _block(count)
    steps = count // block
    scales = [] if weights is None else list(weights)
    copies = 6 if terms == 3 else 4
    lanes = copies // terms if copies % terms == 0 else 1
    copies = lanes * terms
    chunk = math.gcd(rows, 256)

    def body(*refs):
        idx_refs = refs[:terms]
        w_refs = refs[terms : terms + len(scales)]
        val_ref, out_hbm = refs[terms + len(scales) : terms + len(scales) + 2]
        accs = refs[terms + len(scales) + 2 :]

        @pl.when(pl.program_id(0) == 0)
        def _():
            def clear(c, carry):
                for acc in accs:
                    acc[pl.ds(c * chunk, chunk), :] = jnp.zeros((chunk, width), acc.dtype)
                return carry

            lax.fori_loop(0, rows // chunk, clear, 0)

        def step(h, carry):
            for lane in range(lanes):
                g = h * lanes + lane
                row = val_ref[pl.ds(g, 1), :]
                for k in range(terms):
                    add = w_refs[k][g] * row if w_refs else row
                    acc = accs[lane * terms + k]
                    acc[pl.ds(idx_refs[k][g], 1), :] += add
            return carry

        lax.fori_loop(0, block // lanes, step, 0, unroll=unroll)

        @pl.when(pl.program_id(0) == steps - 1)
        def _():
            def fold(c, carry):
                part = pl.ds(c * chunk, chunk)
                total = accs[0][part, :]
                for acc in accs[1:]:
                    total = total + acc[part, :]
                accs[0][part, :] = total
                return carry

            lax.fori_loop(0, rows // chunk, fold, 0)
            pltpu.sync_copy(accs[0], out_hbm)

    smem = pl.BlockSpec((block,), lambda i: (i,), memory_space=pltpu.SMEM)
    return pl.pallas_call(
        body,
        grid=(steps,),
        in_specs=[smem] * (terms + len(scales)) + [pl.BlockSpec((block, width), lambda i: (i, 0))],
        out_specs=pl.BlockSpec(memory_space=pl.ANY),
        out_shape=jax.ShapeDtypeStruct((rows, width), values.dtype),
        scratch_shapes=[pltpu.VMEM((rows, width), values.dtype) for _ in range(copies)],
        compiler_params=pltpu.CompilerParams(
            dimension_semantics=("arbitrary",), vmem_limit_bytes=_vmem_limit(rows, copies)
        ),
    )(*indices, *scales, values)


def extended_2(cells, sides, width):
    for axis, dim in sides:
        count = lax.axis_size(axis)
        head = lax.slice_in_dim(cells, 0, width, axis=dim)
        tail = lax.slice_in_dim(cells, cells.shape[dim] - width, cells.shape[dim], axis=dim)
        cells = jnp.concatenate(
            [
                lax.ppermute(tail, axis, [(i, (i + 1) % count) for i in range(count)]),
                cells,
                lax.ppermute(head, axis, [((i + 1) % count, i) for i in range(count)]),
            ],
            axis=dim,
        )
    return cells


def split_bf16(values):
    kept = lax.reduce_precision(values, exponent_bits=8, mantissa_bits=7)
    return kept.astype(jnp.bfloat16), (values - kept).astype(jnp.bfloat16)


def wave_tables(m_order, points_count):
    points = jnp.arange(points_count, dtype=jnp.int32)
    phase = points[:, None] * m_order[None, :] % points_count
    angle = phase.astype(jnp.float32) * (2.0 * math.pi / points_count)
    return (jnp.cos(angle), jnp.sin(angle))


def on_device(
    eta,
    forcing,
    couplings,
    neighbors,
    halo_send,
    cycle_send,
    stencil,
    stencil_weights,
    m_order,
    lat_weights,
    love,
    legendre,
):
    fields, per_part = eta.shape
    terms = neighbors.shape[0]
    rim_width = halo_send.shape[1] // 2
    band_count = cycle_send.shape[1]
    slot_count = cycle_send.shape[2]
    orders_here = legendre.shape[0]
    lat_count = legendre.shape[2]
    size_x = lax.axis_size("gx")
    size_y = lax.axis_size("gy")
    partitions = size_x * size_y
    cycles_here = lat_count // partitions
    point_count = stencil.shape[1]
    lon_count = point_count // cycles_here
    degrees = m_order.shape[0]
    eta_rows = eta.T
    rim_values = jnp.take(eta, halo_send[0], axis=1)
    padded = extended_2(rim_values, ((("gx", "gy"), 1),), rim_width)
    extended = jnp.concatenate(
        [eta_rows, padded[:, :rim_width].T, padded[:, 3 * rim_width :].T], axis=0
    )
    picked_cells = row_gather([neighbors.reshape(-1)], extended).reshape(terms, per_part, fields)
    change = jnp.zeros(eta_rows.shape, jnp.float32)
    for which in range(terms):
        change = change + couplings[which][:, None] * (picked_cells[which] - eta_rows)
    stepped_rows = eta_rows + change + forcing.T
    outgoing = row_gather([cycle_send[0].reshape(-1)], stepped_rows).reshape(
        band_count, slot_count, fields
    )
    received = lax.all_to_all(outgoing, ("gx", "gy"), split_axis=0, concat_axis=0, tiled=True)
    incoming_rows = received.reshape(-1, fields)
    stencil_rows = [stencil[which] for which in range(terms)]
    weight_rows = [stencil_weights[which] for which in range(terms)]
    gridded_rows = row_gather(stencil_rows, incoming_rows, weight_rows)
    gridded = gridded_rows.T
    cosines, sines = wave_tables(m_order, lon_count)
    table_high, table_low = split_bf16(jnp.concatenate([cosines, sines], axis=1))
    table_high, table_low = lax.optimization_barrier((table_high, table_low))
    scale = lon_count ** (-0.5)
    flat = gridded.reshape(fields * cycles_here, lon_count)
    flat_high, flat_low = split_bf16(flat)
    forward = None
    for left, right in ((flat_high, table_high), (flat_low, table_high), (flat_high, table_low)):
        term = jnp.dot(left, right, preferred_element_type=jnp.float32)
        forward = term if forward is None else forward + term
    fourier = (forward * scale).astype(jnp.bfloat16)
    fourier = fourier.reshape(fields, cycles_here, 2, partitions, orders_here)
    fourier = jnp.transpose(fourier, (3, 4, 2, 0, 1)).reshape(partitions, -1)
    arrived = lax.all_to_all(
        fourier.reshape(partitions, 128, -1), ("gx", "gy"), split_axis=0, concat_axis=0, tiled=True
    )
    arrived = arrived.reshape(partitions, orders_here, 2 * fields, cycles_here)
    spectra = jnp.transpose(arrived, (1, 2, 0, 3)).reshape(orders_here, 2 * fields, lat_count)
    weighted = (spectra.astype(jnp.float32) * lat_weights[None, None, :]).astype(jnp.bfloat16)
    coefficients = jnp.einsum(
        "jci,jli->jcl", weighted, legendre, preferred_element_type=jnp.float32
    )
    scaled = (coefficients * love[None, None, :]).astype(jnp.bfloat16)
    synthesized = jnp.einsum(
        "jcl,jli->jci", scaled, legendre, preferred_element_type=jnp.float32
    ).astype(jnp.bfloat16)
    leaving = synthesized.reshape(orders_here, 2 * fields, partitions, cycles_here)
    leaving = jnp.transpose(leaving, (2, 0, 1, 3)).reshape(partitions, -1)
    returned = lax.all_to_all(
        leaving.reshape(partitions, 128, -1), ("gx", "gy"), split_axis=0, concat_axis=0, tiled=True
    )
    returned = returned.reshape(partitions, orders_here, 2, fields, cycles_here)
    spectral = jnp.transpose(returned, (3, 4, 2, 0, 1)).reshape(fields * cycles_here, 2 * degrees)
    contract = (((1,), (1,)), ((), ()))
    returned_grid = None
    for piece in (table_high, table_low):
        term = lax.dot_general(spectral, piece, contract, preferred_element_type=jnp.float32)
        returned_grid = term if returned_grid is None else returned_grid + term
    grid_rows = (returned_grid * scale).reshape(fields, -1).T
    slot_rows = row_scatter(stencil_rows, grid_rows, band_count * slot_count, weight_rows)
    slot_rows = slot_rows.reshape(band_count, slot_count, fields)
    came_back = lax.all_to_all(slot_rows, ("gx", "gy"), split_axis=0, concat_axis=0, tiled=True)
    homeward = came_back.reshape(-1, fields)
    loading_rows = row_scatter([cycle_send[0].reshape(-1)], homeward, per_part)
    return (stepped_rows.T, loading_rows.T)


def solution(mesh):
    placed = (
        P(None, ("gx", "gy")),
        P(None, ("gx", "gy")),
        P(None, ("gx", "gy")),
        P(None, ("gx", "gy")),
        P(("gx", "gy"), None),
        P(("gx", "gy"), None, None),
        P(None, ("gx", "gy")),
        P(None, ("gx", "gy")),
        P(),
        P(),
        P(),
        P(("gx", "gy"), None, None),
    )
    return jax.shard_map(
        on_device,
        mesh=mesh,
        in_specs=placed,
        out_specs=(P(None, ("gx", "gy")), P(None, ("gx", "gy"))),
        check_vma=False,
    )
```

```python
import math

import jax
import jax.numpy as jnp
from jax import lax
from jax.sharding import PartitionSpec as P


from jax.experimental import pallas as pl
from jax.experimental.pallas import tpu as pltpu


def _block(total, cap=4096):
    size = math.gcd(total, cap)
    return size


def _vmem_limit(table_rows, copies):
    padded = -(-table_rows // 8) * 8 * 128 * 4
    return int(min(copies * padded + (16 << 20), 60 << 20))


def row_gather(indices, table, weights=None, unroll=16):
    rows, width = table.shape
    terms = len(indices)
    count = indices[0].shape[0]
    block = _block(count)
    scales = [] if weights is None else list(weights)

    def body(*refs):
        idx_refs = refs[:terms]
        w_refs = refs[terms : terms + len(scales)]
        tab_hbm, out_ref, tab = refs[terms + len(scales) :]

        @pl.when(pl.program_id(0) == 0)
        def _():
            pltpu.sync_copy(tab_hbm, tab)

        def step(g, carry):
            acc = None
            for k in range(terms):
                row = tab[pl.ds(idx_refs[k][g], 1), :]
                if w_refs:
                    row = w_refs[k][g] * row
                acc = row if acc is None else acc + row
            out_ref[pl.ds(g, 1), :] = acc
            return carry

        lax.fori_loop(0, block, step, 0, unroll=unroll)

    smem = pl.BlockSpec((block,), lambda i: (i,), memory_space=pltpu.SMEM)
    return pl.pallas_call(
        body,
        grid=(count // block,),
        in_specs=[smem] * (terms + len(scales)) + [pl.BlockSpec(memory_space=pl.ANY)],
        out_specs=pl.BlockSpec((block, width), lambda i: (i, 0)),
        out_shape=jax.ShapeDtypeStruct((count, width), table.dtype),
        scratch_shapes=[pltpu.VMEM((rows, width), table.dtype)],
        compiler_params=pltpu.CompilerParams(
            dimension_semantics=("arbitrary",), vmem_limit_bytes=_vmem_limit(rows, 1)
        ),
    )(*indices, *scales, table)


def row_scatter(indices, values, rows, weights=None, unroll=16):
    count, width = values.shape
    terms = len(indices)
    block = _block(count)
    steps = count // block
    scales = [] if weights is None else list(weights)
    copies = 6 if terms == 3 else 4
    lanes = copies // terms if copies % terms == 0 else 1
    copies = lanes * terms
    chunk = math.gcd(rows, 256)

    def body(*refs):
        idx_refs = refs[:terms]
        w_refs = refs[terms : terms + len(scales)]
        val_ref, out_hbm = refs[terms + len(scales) : terms + len(scales) + 2]
        accs = refs[terms + len(scales) + 2 :]

        @pl.when(pl.program_id(0) == 0)
        def _():
            def clear(c, carry):
                for acc in accs:
                    acc[pl.ds(c * chunk, chunk), :] = jnp.zeros((chunk, width), acc.dtype)
                return carry

            lax.fori_loop(0, rows // chunk, clear, 0)

        def step(h, carry):
            for lane in range(lanes):
                g = h * lanes + lane
                row = val_ref[pl.ds(g, 1), :]
                for k in range(terms):
                    add = w_refs[k][g] * row if w_refs else row
                    acc = accs[lane * terms + k]
                    acc[pl.ds(idx_refs[k][g], 1), :] += add
            return carry

        lax.fori_loop(0, block // lanes, step, 0, unroll=unroll)

        @pl.when(pl.program_id(0) == steps - 1)
        def _():
            def fold(c, carry):
                part = pl.ds(c * chunk, chunk)
                total = accs[0][part, :]
                for acc in accs[1:]:
                    total = total + acc[part, :]
                accs[0][part, :] = total
                return carry

            lax.fori_loop(0, rows // chunk, fold, 0)
            pltpu.sync_copy(accs[0], out_hbm)

    smem = pl.BlockSpec((block,), lambda i: (i,), memory_space=pltpu.SMEM)
    return pl.pallas_call(
        body,
        grid=(steps,),
        in_specs=[smem] * (terms + len(scales)) + [pl.BlockSpec((block, width), lambda i: (i, 0))],
        out_specs=pl.BlockSpec(memory_space=pl.ANY),
        out_shape=jax.ShapeDtypeStruct((rows, width), values.dtype),
        scratch_shapes=[pltpu.VMEM((rows, width), values.dtype) for _ in range(copies)],
        compiler_params=pltpu.CompilerParams(
            dimension_semantics=("arbitrary",), vmem_limit_bytes=_vmem_limit(rows, copies)
        ),
    )(*indices, *scales, values)


def legendre_pass(spectra, lat_weights, love, legendre):
    orders, width, lats = spectra.shape
    degrees = legendre.shape[1]

    def body(s_ref, lw_ref, lv_ref, l_ref, o_ref):
        table = l_ref[0]
        weighted = (s_ref[0].astype(jnp.float32) * lw_ref[...]).astype(jnp.bfloat16)
        coefficients = lax.dot_general(
            weighted, table, (((1,), (1,)), ((), ())), preferred_element_type=jnp.float32
        )
        scaled = (coefficients * lv_ref[...]).astype(jnp.bfloat16)
        synthesized = jnp.dot(scaled, table, preferred_element_type=jnp.float32)
        o_ref[0] = synthesized.astype(jnp.bfloat16)

    return pl.pallas_call(
        body,
        grid=(orders,),
        in_specs=[
            pl.BlockSpec((1, width, lats), lambda j: (j, 0, 0)),
            pl.BlockSpec((1, lats), lambda j: (0, 0)),
            pl.BlockSpec((1, degrees), lambda j: (0, 0)),
            pl.BlockSpec((1, degrees, lats), lambda j: (j, 0, 0)),
        ],
        out_specs=pl.BlockSpec((1, width, lats), lambda j: (j, 0, 0)),
        out_shape=jax.ShapeDtypeStruct((orders, width, lats), jnp.bfloat16),
        compiler_params=pltpu.CompilerParams(
            dimension_semantics=("arbitrary",), vmem_limit_bytes=32 << 20
        ),
    )(spectra, lat_weights.reshape(1, -1), love.reshape(1, -1), legendre)


def extended_2(cells, sides, width):
    for axis, dim in sides:
        count = lax.axis_size(axis)
        head = lax.slice_in_dim(cells, 0, width, axis=dim)
        tail = lax.slice_in_dim(cells, cells.shape[dim] - width, cells.shape[dim], axis=dim)
        cells = jnp.concatenate(
            [
                lax.ppermute(tail, axis, [(i, (i + 1) % count) for i in range(count)]),
                cells,
                lax.ppermute(head, axis, [((i + 1) % count, i) for i in range(count)]),
            ],
            axis=dim,
        )
    return cells


def split_bf16(values):
    kept = lax.reduce_precision(values, exponent_bits=8, mantissa_bits=7)
    return kept.astype(jnp.bfloat16), (values - kept).astype(jnp.bfloat16)


def wave_tables(m_order, points_count):
    points = jnp.arange(points_count, dtype=jnp.int32)
    phase = points[:, None] * m_order[None, :] % points_count
    angle = phase.astype(jnp.float32) * (2.0 * math.pi / points_count)
    return (jnp.cos(angle), jnp.sin(angle))


def on_device(
    eta,
    forcing,
    couplings,
    neighbors,
    halo_send,
    cycle_send,
    stencil,
    stencil_weights,
    m_order,
    lat_weights,
    love,
    legendre,
):
    fields, per_part = eta.shape
    terms = neighbors.shape[0]
    rim_width = halo_send.shape[1] // 2
    band_count = cycle_send.shape[1]
    slot_count = cycle_send.shape[2]
    orders_here = legendre.shape[0]
    lat_count = legendre.shape[2]
    size_x = lax.axis_size("gx")
    size_y = lax.axis_size("gy")
    partitions = size_x * size_y
    cycles_here = lat_count // partitions
    point_count = stencil.shape[1]
    lon_count = point_count // cycles_here
    degrees = m_order.shape[0]
    eta_rows = eta.T
    rim_values = jnp.take(eta, halo_send[0], axis=1)
    padded = extended_2(rim_values, ((("gx", "gy"), 1),), rim_width)
    extended = jnp.concatenate(
        [eta_rows, padded[:, :rim_width].T, padded[:, 3 * rim_width :].T], axis=0
    )
    picked_cells = row_gather([neighbors.reshape(-1)], extended).reshape(terms, per_part, fields)
    change = jnp.zeros(eta_rows.shape, jnp.float32)
    for which in range(terms):
        change = change + couplings[which][:, None] * (picked_cells[which] - eta_rows)
    stepped_rows = eta_rows + change + forcing.T
    outgoing = row_gather([cycle_send[0].reshape(-1)], stepped_rows).reshape(
        band_count, slot_count, fields
    )
    received = lax.all_to_all(outgoing, ("gx", "gy"), split_axis=0, concat_axis=0, tiled=True)
    incoming_rows = received.reshape(-1, fields)
    stencil_rows = [stencil[which] for which in range(terms)]
    weight_rows = [stencil_weights[which] for which in range(terms)]
    gridded_rows = row_gather(stencil_rows, incoming_rows, weight_rows)
    gridded = gridded_rows.T
    cosines, sines = wave_tables(m_order, lon_count)
    table_high, table_low = split_bf16(jnp.concatenate([cosines, sines], axis=1))
    table_high, table_low = lax.optimization_barrier((table_high, table_low))
    scale = lon_count ** (-0.5)
    flat = gridded.reshape(fields * cycles_here, lon_count)
    flat_high, flat_low = split_bf16(flat)
    forward = None
    for left, right in ((flat_high, table_high), (flat_low, table_high), (flat_high, table_low)):
        term = jnp.dot(left, right, preferred_element_type=jnp.float32)
        forward = term if forward is None else forward + term
    fourier = (forward * scale).astype(jnp.bfloat16)
    fourier = fourier.reshape(fields, cycles_here, 2, partitions, orders_here)
    fourier = jnp.transpose(fourier, (3, 4, 2, 0, 1)).reshape(partitions, -1)
    arrived = lax.all_to_all(
        fourier.reshape(partitions, 128, -1), ("gx", "gy"), split_axis=0, concat_axis=0, tiled=True
    )
    arrived = arrived.reshape(partitions, orders_here, 2 * fields, cycles_here)
    spectra = jnp.transpose(arrived, (1, 2, 0, 3)).reshape(orders_here, 2 * fields, lat_count)
    synthesized = legendre_pass(spectra, lat_weights, love, legendre)
    leaving = synthesized.reshape(orders_here, 2 * fields, partitions, cycles_here)
    leaving = jnp.transpose(leaving, (2, 0, 1, 3)).reshape(partitions, -1)
    returned = lax.all_to_all(
        leaving.reshape(partitions, 128, -1), ("gx", "gy"), split_axis=0, concat_axis=0, tiled=True
    )
    returned = returned.reshape(partitions, orders_here, 2, fields, cycles_here)
    spectral = jnp.transpose(returned, (3, 4, 2, 0, 1)).reshape(fields * cycles_here, 2 * degrees)
    contract = (((1,), (1,)), ((), ()))
    returned_grid = None
    for piece in (table_high, table_low):
        term = lax.dot_general(spectral, piece, contract, preferred_element_type=jnp.float32)
        returned_grid = term if returned_grid is None else returned_grid + term
    grid_rows = (returned_grid * scale).reshape(fields, -1).T
    slot_rows = row_scatter(stencil_rows, grid_rows, band_count * slot_count, weight_rows)
    slot_rows = slot_rows.reshape(band_count, slot_count, fields)
    came_back = lax.all_to_all(slot_rows, ("gx", "gy"), split_axis=0, concat_axis=0, tiled=True)
    homeward = came_back.reshape(-1, fields)
    loading_rows = row_scatter([cycle_send[0].reshape(-1)], homeward, per_part)
    return (stepped_rows.T, loading_rows.T)


def solution(mesh):
    placed = (
        P(None, ("gx", "gy")),
        P(None, ("gx", "gy")),
        P(None, ("gx", "gy")),
        P(None, ("gx", "gy")),
        P(("gx", "gy"), None),
        P(("gx", "gy"), None, None),
        P(None, ("gx", "gy")),
        P(None, ("gx", "gy")),
        P(),
        P(),
        P(),
        P(("gx", "gy"), None, None),
    )
    return jax.shard_map(
        on_device,
        mesh=mesh,
        in_specs=placed,
        out_specs=(P(None, ("gx", "gy")), P(None, ("gx", "gy"))),
        check_vma=False,
    )
```

```python
import math

import jax
import jax.numpy as jnp
from jax import lax
from jax.sharding import PartitionSpec as P


from jax.experimental import pallas as pl
from jax.experimental.pallas import tpu as pltpu


def _block(total, cap=4096):
    size = math.gcd(total, cap)
    return size


def _vmem_limit(table_rows, copies):
    padded = -(-table_rows // 8) * 8 * 128 * 4
    return int(min(copies * padded + (16 << 20), 60 << 20))


def row_gather(indices, table, weights=None, unroll=16):
    rows, width = table.shape
    terms = len(indices)
    count = indices[0].shape[0]
    block = _block(count)
    scales = [] if weights is None else list(weights)

    def body(*refs):
        idx_refs = refs[:terms]
        w_refs = refs[terms : terms + len(scales)]
        tab_hbm, out_ref, tab = refs[terms + len(scales) :]

        @pl.when(pl.program_id(0) == 0)
        def _():
            pltpu.sync_copy(tab_hbm, tab)

        def step(g, carry):
            acc = None
            for k in range(terms):
                row = tab[pl.ds(idx_refs[k][g], 1), :]
                if w_refs:
                    row = w_refs[k][g] * row
                acc = row if acc is None else acc + row
            out_ref[pl.ds(g, 1), :] = acc
            return carry

        lax.fori_loop(0, block, step, 0, unroll=unroll)

    smem = pl.BlockSpec((block,), lambda i: (i,), memory_space=pltpu.SMEM)
    return pl.pallas_call(
        body,
        grid=(count // block,),
        in_specs=[smem] * (terms + len(scales)) + [pl.BlockSpec(memory_space=pl.ANY)],
        out_specs=pl.BlockSpec((block, width), lambda i: (i, 0)),
        out_shape=jax.ShapeDtypeStruct((count, width), table.dtype),
        scratch_shapes=[pltpu.VMEM((rows, width), table.dtype)],
        compiler_params=pltpu.CompilerParams(
            dimension_semantics=("arbitrary",), vmem_limit_bytes=_vmem_limit(rows, 1)
        ),
    )(*indices, *scales, table)


def row_scatter(indices, values, rows, weights=None, unroll=16):
    count, width = values.shape
    terms = len(indices)
    block = _block(count)
    steps = count // block
    scales = [] if weights is None else list(weights)
    copies = 6 if terms == 3 else 4
    lanes = copies // terms if copies % terms == 0 else 1
    copies = lanes * terms
    chunk = math.gcd(rows, 256)

    def body(*refs):
        idx_refs = refs[:terms]
        w_refs = refs[terms : terms + len(scales)]
        val_ref, out_hbm = refs[terms + len(scales) : terms + len(scales) + 2]
        accs = refs[terms + len(scales) + 2 :]

        @pl.when(pl.program_id(0) == 0)
        def _():
            def clear(c, carry):
                for acc in accs:
                    acc[pl.ds(c * chunk, chunk), :] = jnp.zeros((chunk, width), acc.dtype)
                return carry

            lax.fori_loop(0, rows // chunk, clear, 0)

        def step(h, carry):
            for lane in range(lanes):
                g = h * lanes + lane
                row = val_ref[pl.ds(g, 1), :]
                for k in range(terms):
                    add = w_refs[k][g] * row if w_refs else row
                    acc = accs[lane * terms + k]
                    acc[pl.ds(idx_refs[k][g], 1), :] += add
            return carry

        lax.fori_loop(0, block // lanes, step, 0, unroll=unroll)

        @pl.when(pl.program_id(0) == steps - 1)
        def _():
            def fold(c, carry):
                part = pl.ds(c * chunk, chunk)
                total = accs[0][part, :]
                for acc in accs[1:]:
                    total = total + acc[part, :]
                accs[0][part, :] = total
                return carry

            lax.fori_loop(0, rows // chunk, fold, 0)
            pltpu.sync_copy(accs[0], out_hbm)

    smem = pl.BlockSpec((block,), lambda i: (i,), memory_space=pltpu.SMEM)
    return pl.pallas_call(
        body,
        grid=(steps,),
        in_specs=[smem] * (terms + len(scales)) + [pl.BlockSpec((block, width), lambda i: (i, 0))],
        out_specs=pl.BlockSpec(memory_space=pl.ANY),
        out_shape=jax.ShapeDtypeStruct((rows, width), values.dtype),
        scratch_shapes=[pltpu.VMEM((rows, width), values.dtype) for _ in range(copies)],
        compiler_params=pltpu.CompilerParams(
            dimension_semantics=("arbitrary",), vmem_limit_bytes=_vmem_limit(rows, copies)
        ),
    )(*indices, *scales, values)


def legendre_pass(spectra, lat_weights, love, legendre):
    orders, width, lats = spectra.shape
    degrees = legendre.shape[1]

    def body(s_ref, lw_ref, lv_ref, l_ref, o_ref):
        table = l_ref[0]
        weighted = (s_ref[0].astype(jnp.float32) * lw_ref[...]).astype(jnp.bfloat16)
        coefficients = lax.dot_general(
            weighted, table, (((1,), (1,)), ((), ())), preferred_element_type=jnp.float32
        )
        scaled = (coefficients * lv_ref[...]).astype(jnp.bfloat16)
        synthesized = jnp.dot(scaled, table, preferred_element_type=jnp.float32)
        o_ref[0] = synthesized.astype(jnp.bfloat16)

    return pl.pallas_call(
        body,
        grid=(orders,),
        in_specs=[
            pl.BlockSpec((1, width, lats), lambda j: (j, 0, 0)),
            pl.BlockSpec((1, lats), lambda j: (0, 0)),
            pl.BlockSpec((1, degrees), lambda j: (0, 0)),
            pl.BlockSpec((1, degrees, lats), lambda j: (j, 0, 0)),
        ],
        out_specs=pl.BlockSpec((1, width, lats), lambda j: (j, 0, 0)),
        out_shape=jax.ShapeDtypeStruct((orders, width, lats), jnp.bfloat16),
        compiler_params=pltpu.CompilerParams(
            dimension_semantics=("arbitrary",), vmem_limit_bytes=32 << 20
        ),
    )(spectra, lat_weights.reshape(1, -1), love.reshape(1, -1), legendre)


def extended_2(cells, sides, width):
    for axis, dim in sides:
        count = lax.axis_size(axis)
        head = lax.slice_in_dim(cells, 0, width, axis=dim)
        tail = lax.slice_in_dim(cells, cells.shape[dim] - width, cells.shape[dim], axis=dim)
        cells = jnp.concatenate(
            [
                lax.ppermute(tail, axis, [(i, (i + 1) % count) for i in range(count)]),
                cells,
                lax.ppermute(head, axis, [((i + 1) % count, i) for i in range(count)]),
            ],
            axis=dim,
        )
    return cells


def split_bf16(values):
    kept = lax.reduce_precision(values, exponent_bits=8, mantissa_bits=7)
    return kept.astype(jnp.bfloat16), (values - kept).astype(jnp.bfloat16)


def wave_tables(m_order, points_count):
    half = points_count // 2
    points = jnp.arange(half + 1, dtype=jnp.int32)
    phase = points[:, None] * m_order[None, :] % points_count
    angle = phase.astype(jnp.float32) * (2.0 * math.pi / points_count)
    cos_half, sin_half = jnp.cos(angle), jnp.sin(angle)
    cos_rest = jnp.flip(cos_half[1:half], axis=0)
    sin_rest = jnp.flip(sin_half[1:half], axis=0)
    return (
        jnp.concatenate([cos_half, cos_rest], axis=0),
        jnp.concatenate([sin_half, -sin_rest], axis=0),
    )


def on_device(
    eta,
    forcing,
    couplings,
    neighbors,
    halo_send,
    cycle_send,
    stencil,
    stencil_weights,
    m_order,
    lat_weights,
    love,
    legendre,
):
    fields, per_part = eta.shape
    terms = neighbors.shape[0]
    rim_width = halo_send.shape[1] // 2
    band_count = cycle_send.shape[1]
    slot_count = cycle_send.shape[2]
    orders_here = legendre.shape[0]
    lat_count = legendre.shape[2]
    size_x = lax.axis_size("gx")
    size_y = lax.axis_size("gy")
    partitions = size_x * size_y
    cycles_here = lat_count // partitions
    point_count = stencil.shape[1]
    lon_count = point_count // cycles_here
    degrees = m_order.shape[0]
    eta_rows = eta.T
    rim_values = jnp.take(eta, halo_send[0], axis=1)
    padded = extended_2(rim_values, ((("gx", "gy"), 1),), rim_width)
    extended = jnp.concatenate(
        [eta_rows, padded[:, :rim_width].T, padded[:, 3 * rim_width :].T], axis=0
    )
    picked_cells = row_gather([neighbors.reshape(-1)], extended).reshape(terms, per_part, fields)
    change = jnp.zeros(eta_rows.shape, jnp.float32)
    for which in range(terms):
        change = change + couplings[which][:, None] * (picked_cells[which] - eta_rows)
    stepped_rows = eta_rows + change + forcing.T
    outgoing = row_gather([cycle_send[0].reshape(-1)], stepped_rows).reshape(
        band_count, slot_count, fields
    )
    received = lax.all_to_all(outgoing, ("gx", "gy"), split_axis=0, concat_axis=0, tiled=True)
    incoming_rows = received.reshape(-1, fields)
    stencil_rows = [stencil[which] for which in range(terms)]
    weight_rows = [stencil_weights[which] for which in range(terms)]
    gridded_rows = row_gather(stencil_rows, incoming_rows, weight_rows)
    gridded = gridded_rows.T
    cosines, sines = wave_tables(m_order, lon_count)
    table_high, table_low = split_bf16(jnp.concatenate([cosines, sines], axis=1))
    table_high, table_low = lax.optimization_barrier((table_high, table_low))
    scale = lon_count ** (-0.5)
    flat = gridded.reshape(fields * cycles_here, lon_count)
    flat_high, flat_low = split_bf16(flat)
    forward = None
    for left, right in ((flat_high, table_high), (flat_low, table_high), (flat_high, table_low)):
        term = jnp.dot(left, right, preferred_element_type=jnp.float32)
        forward = term if forward is None else forward + term
    fourier = (forward * scale).astype(jnp.bfloat16)
    fourier = fourier.reshape(fields, cycles_here, 2, partitions, orders_here)
    fourier = jnp.transpose(fourier, (3, 4, 2, 0, 1)).reshape(partitions, -1)
    arrived = lax.all_to_all(
        fourier.reshape(partitions, 128, -1), ("gx", "gy"), split_axis=0, concat_axis=0, tiled=True
    )
    arrived = arrived.reshape(partitions, orders_here, 2 * fields, cycles_here)
    spectra = jnp.transpose(arrived, (1, 2, 0, 3)).reshape(orders_here, 2 * fields, lat_count)
    synthesized = legendre_pass(spectra, lat_weights, love, legendre)
    leaving = synthesized.reshape(orders_here, 2 * fields, partitions, cycles_here)
    leaving = jnp.transpose(leaving, (2, 0, 1, 3)).reshape(partitions, -1)
    returned = lax.all_to_all(
        leaving.reshape(partitions, 128, -1), ("gx", "gy"), split_axis=0, concat_axis=0, tiled=True
    )
    returned = returned.reshape(partitions, orders_here, 2, fields, cycles_here)
    spectral = jnp.transpose(returned, (3, 4, 2, 0, 1)).reshape(fields * cycles_here, 2 * degrees)
    contract = (((1,), (1,)), ((), ()))
    returned_grid = None
    for piece in (table_high, table_low):
        term = lax.dot_general(spectral, piece, contract, preferred_element_type=jnp.float32)
        returned_grid = term if returned_grid is None else returned_grid + term
    grid_rows = (returned_grid * scale).reshape(fields, -1).T
    slot_rows = row_scatter(stencil_rows, grid_rows, band_count * slot_count, weight_rows)
    slot_rows = slot_rows.reshape(band_count, slot_count, fields)
    came_back = lax.all_to_all(slot_rows, ("gx", "gy"), split_axis=0, concat_axis=0, tiled=True)
    homeward = came_back.reshape(-1, fields)
    loading_rows = row_scatter([cycle_send[0].reshape(-1)], homeward, per_part)
    return (stepped_rows.T, loading_rows.T)


def solution(mesh):
    placed = (
        P(None, ("gx", "gy")),
        P(None, ("gx", "gy")),
        P(None, ("gx", "gy")),
        P(None, ("gx", "gy")),
        P(("gx", "gy"), None),
        P(("gx", "gy"), None, None),
        P(None, ("gx", "gy")),
        P(None, ("gx", "gy")),
        P(),
        P(),
        P(),
        P(("gx", "gy"), None, None),
    )
    return jax.shard_map(
        on_device,
        mesh=mesh,
        in_specs=placed,
        out_specs=(P(None, ("gx", "gy")), P(None, ("gx", "gy"))),
        check_vma=False,
    )
```

```python
import math

import jax
import jax.numpy as jnp
from jax import lax
from jax.sharding import PartitionSpec as P


from jax.experimental import pallas as pl
from jax.experimental.pallas import tpu as pltpu


def _block(total, cap=4096):
    size = math.gcd(total, cap)
    return size


def _vmem_limit(table_rows, copies):
    padded = -(-table_rows // 8) * 8 * 128 * 4
    return int(min(copies * padded + (16 << 20), 60 << 20))


def row_gather(indices, table, weights=None, unroll=32):
    rows, width = table.shape
    terms = len(indices)
    count = indices[0].shape[0]
    block = _block(count)
    scales = [] if weights is None else list(weights)

    def body(*refs):
        idx_refs = refs[:terms]
        w_refs = refs[terms : terms + len(scales)]
        tab_hbm, out_ref, tab = refs[terms + len(scales) :]

        @pl.when(pl.program_id(0) == 0)
        def _():
            pltpu.sync_copy(tab_hbm, tab)

        def step(g, carry):
            acc = None
            for k in range(terms):
                row = tab[pl.ds(idx_refs[k][g], 1), :]
                if w_refs:
                    row = w_refs[k][g] * row
                acc = row if acc is None else acc + row
            out_ref[pl.ds(g, 1), :] = acc
            return carry

        lax.fori_loop(0, block, step, 0, unroll=unroll)

    smem = pl.BlockSpec((block,), lambda i: (i,), memory_space=pltpu.SMEM)
    return pl.pallas_call(
        body,
        grid=(count // block,),
        in_specs=[smem] * (terms + len(scales)) + [pl.BlockSpec(memory_space=pl.ANY)],
        out_specs=pl.BlockSpec((block, width), lambda i: (i, 0)),
        out_shape=jax.ShapeDtypeStruct((count, width), table.dtype),
        scratch_shapes=[pltpu.VMEM((rows, width), table.dtype)],
        compiler_params=pltpu.CompilerParams(
            dimension_semantics=("arbitrary",), vmem_limit_bytes=_vmem_limit(rows, 1)
        ),
    )(*indices, *scales, table)


def row_scatter(indices, values, rows, weights=None, unroll=16):
    count, width = values.shape
    terms = len(indices)
    block = _block(count)
    steps = count // block
    scales = [] if weights is None else list(weights)
    copies = 6 if terms == 3 else 4
    lanes = copies // terms if copies % terms == 0 else 1
    copies = lanes * terms
    chunk = math.gcd(rows, 256)

    def body(*refs):
        idx_refs = refs[:terms]
        w_refs = refs[terms : terms + len(scales)]
        val_ref, out_hbm = refs[terms + len(scales) : terms + len(scales) + 2]
        accs = refs[terms + len(scales) + 2 :]

        @pl.when(pl.program_id(0) == 0)
        def _():
            def clear(c, carry):
                for acc in accs:
                    acc[pl.ds(c * chunk, chunk), :] = jnp.zeros((chunk, width), acc.dtype)
                return carry

            lax.fori_loop(0, rows // chunk, clear, 0)

        def step(h, carry):
            for lane in range(lanes):
                g = h * lanes + lane
                row = val_ref[pl.ds(g, 1), :]
                for k in range(terms):
                    add = w_refs[k][g] * row if w_refs else row
                    acc = accs[lane * terms + k]
                    acc[pl.ds(idx_refs[k][g], 1), :] += add
            return carry

        lax.fori_loop(0, block // lanes, step, 0, unroll=unroll)

        @pl.when(pl.program_id(0) == steps - 1)
        def _():
            def fold(c, carry):
                part = pl.ds(c * chunk, chunk)
                total = accs[0][part, :]
                for acc in accs[1:]:
                    total = total + acc[part, :]
                accs[0][part, :] = total
                return carry

            lax.fori_loop(0, rows // chunk, fold, 0)
            pltpu.sync_copy(accs[0], out_hbm)

    smem = pl.BlockSpec((block,), lambda i: (i,), memory_space=pltpu.SMEM)
    return pl.pallas_call(
        body,
        grid=(steps,),
        in_specs=[smem] * (terms + len(scales)) + [pl.BlockSpec((block, width), lambda i: (i, 0))],
        out_specs=pl.BlockSpec(memory_space=pl.ANY),
        out_shape=jax.ShapeDtypeStruct((rows, width), values.dtype),
        scratch_shapes=[pltpu.VMEM((rows, width), values.dtype) for _ in range(copies)],
        compiler_params=pltpu.CompilerParams(
            dimension_semantics=("arbitrary",), vmem_limit_bytes=_vmem_limit(rows, copies)
        ),
    )(*indices, *scales, values)


def legendre_pass(spectra, lat_weights, love, legendre):
    orders, width, lats = spectra.shape
    degrees = legendre.shape[1]

    def body(s_ref, lw_ref, lv_ref, l_ref, o_ref):
        table = l_ref[0]
        weighted = (s_ref[0].astype(jnp.float32) * lw_ref[...]).astype(jnp.bfloat16)
        coefficients = lax.dot_general(
            weighted, table, (((1,), (1,)), ((), ())), preferred_element_type=jnp.float32
        )
        scaled = (coefficients * lv_ref[...]).astype(jnp.bfloat16)
        synthesized = jnp.dot(scaled, table, preferred_element_type=jnp.float32)
        o_ref[0] = synthesized.astype(jnp.bfloat16)

    return pl.pallas_call(
        body,
        grid=(orders,),
        in_specs=[
            pl.BlockSpec((1, width, lats), lambda j: (j, 0, 0)),
            pl.BlockSpec((1, lats), lambda j: (0, 0)),
            pl.BlockSpec((1, degrees), lambda j: (0, 0)),
            pl.BlockSpec((1, degrees, lats), lambda j: (j, 0, 0)),
        ],
        out_specs=pl.BlockSpec((1, width, lats), lambda j: (j, 0, 0)),
        out_shape=jax.ShapeDtypeStruct((orders, width, lats), jnp.bfloat16),
        compiler_params=pltpu.CompilerParams(
            dimension_semantics=("arbitrary",), vmem_limit_bytes=32 << 20
        ),
    )(spectra, lat_weights.reshape(1, -1), love.reshape(1, -1), legendre)


def extended_2(cells, sides, width):
    for axis, dim in sides:
        count = lax.axis_size(axis)
        head = lax.slice_in_dim(cells, 0, width, axis=dim)
        tail = lax.slice_in_dim(cells, cells.shape[dim] - width, cells.shape[dim], axis=dim)
        cells = jnp.concatenate(
            [
                lax.ppermute(tail, axis, [(i, (i + 1) % count) for i in range(count)]),
                cells,
                lax.ppermute(head, axis, [((i + 1) % count, i) for i in range(count)]),
            ],
            axis=dim,
        )
    return cells


def split_bf16(values):
    kept = lax.reduce_precision(values, exponent_bits=8, mantissa_bits=7)
    return kept.astype(jnp.bfloat16), (values - kept).astype(jnp.bfloat16)


def wave_tables(m_order, points_count):
    points = jnp.arange(points_count, dtype=jnp.int32)
    phase = points[:, None] * m_order[None, :] % points_count
    angle = phase.astype(jnp.float32) * (2.0 * math.pi / points_count)
    return (jnp.cos(angle), jnp.sin(angle))


def on_device(
    eta,
    forcing,
    couplings,
    neighbors,
    halo_send,
    cycle_send,
    stencil,
    stencil_weights,
    m_order,
    lat_weights,
    love,
    legendre,
):
    fields, per_part = eta.shape
    terms = neighbors.shape[0]
    rim_width = halo_send.shape[1] // 2
    band_count = cycle_send.shape[1]
    slot_count = cycle_send.shape[2]
    orders_here = legendre.shape[0]
    lat_count = legendre.shape[2]
    size_x = lax.axis_size("gx")
    size_y = lax.axis_size("gy")
    partitions = size_x * size_y
    cycles_here = lat_count // partitions
    point_count = stencil.shape[1]
    lon_count = point_count // cycles_here
    degrees = m_order.shape[0]
    eta_rows = eta.T
    rim_values = jnp.take(eta, halo_send[0], axis=1)
    padded = extended_2(rim_values, ((("gx", "gy"), 1),), rim_width)
    extended = jnp.concatenate(
        [eta_rows, padded[:, :rim_width].T, padded[:, 3 * rim_width :].T], axis=0
    )
    picked_cells = row_gather([neighbors.reshape(-1)], extended).reshape(terms, per_part, fields)
    change = jnp.zeros(eta_rows.shape, jnp.float32)
    for which in range(terms):
        change = change + couplings[which][:, None] * (picked_cells[which] - eta_rows)
    stepped_rows = eta_rows + change + forcing.T
    outgoing = row_gather([cycle_send[0].reshape(-1)], stepped_rows).reshape(
        band_count, slot_count, fields
    )
    received = lax.all_to_all(outgoing, ("gx", "gy"), split_axis=0, concat_axis=0, tiled=True)
    incoming_rows = received.reshape(-1, fields)
    stencil_rows = [stencil[which] for which in range(terms)]
    weight_rows = [stencil_weights[which] for which in range(terms)]
    gridded_rows = row_gather(stencil_rows, incoming_rows, weight_rows)
    gridded = gridded_rows.T
    cosines, sines = wave_tables(m_order, lon_count)
    table_high, table_low = split_bf16(jnp.concatenate([cosines, sines], axis=1))
    table_high, table_low = lax.optimization_barrier((table_high, table_low))
    scale = lon_count ** (-0.5)
    flat = gridded.reshape(fields * cycles_here, lon_count)
    flat_high, flat_low = split_bf16(flat)
    forward = None
    for left, right in ((flat_high, table_high), (flat_low, table_high), (flat_high, table_low)):
        term = jnp.dot(left, right, preferred_element_type=jnp.float32)
        forward = term if forward is None else forward + term
    fourier = (forward * scale).astype(jnp.bfloat16)
    fourier = fourier.reshape(fields, cycles_here, 2, partitions, orders_here)
    fourier = jnp.transpose(fourier, (3, 4, 2, 0, 1)).reshape(partitions, -1)
    arrived = lax.all_to_all(
        fourier.reshape(partitions, 128, -1), ("gx", "gy"), split_axis=0, concat_axis=0, tiled=True
    )
    arrived = arrived.reshape(partitions, orders_here, 2 * fields, cycles_here)
    spectra = jnp.transpose(arrived, (1, 2, 0, 3)).reshape(orders_here, 2 * fields, lat_count)
    synthesized = legendre_pass(spectra, lat_weights, love, legendre)
    leaving = synthesized.reshape(orders_here, 2 * fields, partitions, cycles_here)
    leaving = jnp.transpose(leaving, (2, 0, 1, 3)).reshape(partitions, -1)
    returned = lax.all_to_all(
        leaving.reshape(partitions, 128, -1), ("gx", "gy"), split_axis=0, concat_axis=0, tiled=True
    )
    returned = returned.reshape(partitions, orders_here, 2, fields, cycles_here)
    spectral = jnp.transpose(returned, (3, 4, 2, 0, 1)).reshape(fields * cycles_here, 2 * degrees)
    contract = (((1,), (1,)), ((), ()))
    returned_grid = None
    for piece in (table_high, table_low):
        term = lax.dot_general(spectral, piece, contract, preferred_element_type=jnp.float32)
        returned_grid = term if returned_grid is None else returned_grid + term
    grid_rows = (returned_grid * scale).reshape(fields, -1).T
    slot_rows = row_scatter(stencil_rows, grid_rows, band_count * slot_count, weight_rows)
    slot_rows = slot_rows.reshape(band_count, slot_count, fields)
    came_back = lax.all_to_all(slot_rows, ("gx", "gy"), split_axis=0, concat_axis=0, tiled=True)
    homeward = came_back.reshape(-1, fields)
    loading_rows = row_scatter([cycle_send[0].reshape(-1)], homeward, per_part)
    return (stepped_rows.T, loading_rows.T)


def solution(mesh):
    placed = (
        P(None, ("gx", "gy")),
        P(None, ("gx", "gy")),
        P(None, ("gx", "gy")),
        P(None, ("gx", "gy")),
        P(("gx", "gy"), None),
        P(("gx", "gy"), None, None),
        P(None, ("gx", "gy")),
        P(None, ("gx", "gy")),
        P(),
        P(),
        P(),
        P(("gx", "gy"), None, None),
    )
    return jax.shard_map(
        on_device,
        mesh=mesh,
        in_specs=placed,
        out_specs=(P(None, ("gx", "gy")), P(None, ("gx", "gy"))),
        check_vma=False,
    )
```
